128 devices in a mesh: tile: 8 (over x, core), orient: 16 (over z, y).
Axes of the slice: x: 4, y: 4, z: 4, core: 2. Of those that a mesh axis runs over, the one named last changes fastest.
Arguments:
- micrograph: float32 [4096, 512], P('tile'), may hold values from -40 to 40
- templates: float32 [16, 256, 256], P('orient', 'tile'), may hold values from -6 to 6
- defocus_values: float32 [4], replicated, may hold values from 5000 to 20000
- defocus_group: int32 [8], P('tile'), may hold values from 0 to 3, as said below
Outputs:
- best_score: float32 [4096, 512], P(('tile', 'orient'))
- second_score: float32 [4096, 512], P(('tile', 'orient'))
- mean_score: float32 [4096, 512], P(('tile', 'orient'))
- score_variance: float32 [4096, 512], P(('tile', 'orient'))
The draws below stay inside these ranges and needn't reach their ends.
Inputs may be any that keep to these rules, and one draw needn't show every extreme that they name: `defocus_group`: every group is used by some tile.
All inputs are finite; a program needn't handle non-finite values.
Results may differ from the reference program's by a relative error of at most 0.0003.
Values sent between devices are 32-bit elements; how exact they have to be, the bound alone decides.
No kernel may reach another device: no remote copies, remote signals or barrier semaphores. Data moves between devices by JAX's collectives and lax.ppermute only.
A program may use at most 128 MiB of HBM per device.

```python
import math
import jax
import jax.numpy as jnp
from jax import lax

TS = 512
TPL = 256
GROUPS = 4
TILES = 8
ORIENTS = 16
ROWS = 4096


def draw_micrograph(key, part):
    key_noise = jax.random.fold_in(key, 0)
    last_tile = max(ROWS // TS - 1, 1)
    fraction = (jnp.arange(ROWS) // TS).astype(jnp.float32) / last_tile
    factor = jnp.exp(math.log(3.0) * fraction)[:, None]
    offset = (0.2 + 0.6 * fraction)[:, None]
    noise_map = jax.random.truncated_normal(key_noise, -4.0, 4.0, (ROWS, TS), jnp.float32)
    return (noise_map * factor + offset).astype(jnp.float32)


def draw_defocus_group(key, part):
    order = jax.random.permutation(jax.random.fold_in(key, 7), TILES)
    return (order % GROUPS).astype(jnp.int32)


def block_levels(own_key, dims, shards, least, largest):
    loudness, own = 1.0, jax.random.fold_in(own_key, 6)
    for dim, blocks in shards:
        draws = jnp.exp(jax.random.uniform(jax.random.fold_in(own, dim), (blocks,), jnp.float32, least / len(shards), largest / len(shards)))
        loudness = loudness * jnp.repeat(draws, dims[dim] // blocks).reshape([-1 if axis == dim else 1 for axis in range(len(dims))])
    return loudness


def gaussian(key, extent, scale, limit, cuts=(), kind=jnp.bfloat16):
    result = scale * jax.random.normal(key, extent, jnp.float32)
    if cuts:
        result = result * block_levels(key, extent, cuts, -0.22, 0.18)
    return jnp.clip(result, -limit, limit).astype(kind)


def setup_inputs(seed: int = 0) -> dict:
    seeds = jax.random.split(jax.random.key(seed), 5)
    return {
        "micrograph": draw_micrograph(jax.random.fold_in(seeds[4], 71), 0),
        "templates": gaussian(seeds[1], (ORIENTS, TPL, TPL), 1.0, 6.0, ((0, 16), (1, 8)), jnp.float32),
        "defocus_values": jnp.clip(jax.random.uniform(seeds[2], (GROUPS,), jnp.float32, 5000.0, 20000.0), 5000.0, 20000.0),
        "defocus_group": draw_defocus_group(jax.random.fold_in(seeds[4], 71), 0),
    }


WAVELENGTH = 0.0197
AMPLITUDE = 0.07

def reference(micrograph, templates, defocus_values, defocus_group):
    margin = TPL // 2
    ext_size = TS + TPL
    pixel_count = ROWS * TS
    centre = jnp.sum(micrograph) / pixel_count
    mean_square = jnp.sum(micrograph * micrograph) / pixel_count
    spread = jnp.sqrt(mean_square - centre * centre + 1e-05)
    normal_image = (micrograph - centre) / spread
    padded = jnp.pad(normal_image, margin)
    centred = templates - lax.optimization_barrier(jnp.mean(templates, axis=(1, 2), keepdims=True))
    root_mean = jnp.sqrt(lax.optimization_barrier(jnp.mean(centred * centred, axis=(1, 2), keepdims=True)) + 1e-06)
    normed = centred / (root_mean * TPL)
    tmpl_spec = jnp.conj(jnp.fft.fft2(jnp.pad(normed, ((0, 0), (0, ext_size - TPL), (0, ext_size - TPL)))))
    positions = jnp.arange(ext_size, dtype=jnp.int32)
    frequency = jnp.where(positions < ext_size // 2, positions, positions - ext_size).astype(jnp.float32) / ext_size
    freq_square = frequency[:, None] ** 2 + frequency[None, :] ** 2

    def one_tile(tile_index):
        window = lax.dynamic_slice(padded, (tile_index * TS, jnp.zeros((), jnp.int32)), (ext_size, ext_size))
        defocus = defocus_values[defocus_group[tile_index]]
        phase_shift = math.pi * WAVELENGTH * defocus * freq_square
        contrast = -(math.sqrt(1.0 - AMPLITUDE * AMPLITUDE) * jnp.sin(phase_shift) + AMPLITUDE * jnp.cos(phase_shift))
        product_spec = jnp.fft.fft2(window)[None] * tmpl_spec * contrast[None]
        scores = jnp.real(jnp.fft.ifft2(product_spec))[:, :TS, :TS]
        ranked = lax.top_k(jnp.moveaxis(scores, 0, -1), 2)[0]
        sum_scores = lax.optimization_barrier(jnp.sum(scores, axis=0))
        squares = lax.optimization_barrier(jnp.sum(scores * scores, axis=0))
        mean_map = sum_scores / ORIENTS
        variance = squares / ORIENTS - mean_map * mean_map
        return (ranked[..., 0], ranked[..., 1], mean_map, variance)
    results = lax.map(one_tile, jnp.arange(TILES, dtype=jnp.int32))
    return (results[0].reshape(ROWS, TS), results[1].reshape(ROWS, TS), results[2].reshape(ROWS, TS), results[3].reshape(ROWS, TS))
```

```python
import math

import numpy as np
import jax
import jax.numpy as jnp
from jax import lax
from jax.sharding import PartitionSpec as P

TPL = 256


WAVELENGTH = 0.0197
AMPLITUDE = 0.07
mode = lax.Precision.HIGH


def padded(shard, sides, width):
    for axis, dim in sides:
        size, length = (lax.axis_size(axis), shard.shape[dim])
        up = [(i, (i + 1) % size) for i in range(size - 1)]
        down = [(j, i) for i, j in up]
        last = lax.slice_in_dim(shard, length - width, length, axis=dim)
        initial = lax.slice_in_dim(shard, 0, width, axis=dim)
        before = lax.ppermute(last, axis, up)
        after = lax.ppermute(initial, axis, down)
        shard = jnp.concatenate([before, shard, after], axis=dim)
    return shard


def product(former, latter):
    return jnp.dot(former, latter, precision=mode, preferred_element_type=jnp.float32)


def tables(tile_width, margin, extent):
    n = tile_width + 2 * margin
    h = n // 2 + 1
    idx = np.arange(n)
    angles = 2.0 * np.pi * ((idx[:, None] * idx[None, :]) % n) / n
    cos, sin = np.cos(angles), np.sin(angles)
    left = np.concatenate([cos[:h], sin[:h]], axis=0)
    left_t = left[:, :extent]
    right_w = np.concatenate([cos[margin:margin + tile_width], sin[margin:margin + tile_width]], axis=1)
    right_t = np.concatenate([cos[:extent], sin[:extent]], axis=1)
    back = np.concatenate([cos[:, :tile_width], sin[:, :tile_width]], axis=1)
    weight = np.full(h, 2.0)
    weight[0] = 1.0
    weight[-1] = 1.0
    final = np.concatenate(
        [cos[:tile_width, :h] * weight, -2.0 * sin[:tile_width, 1:h - 1]], axis=1
    ) / (n * n)
    as32 = lambda a: jnp.asarray(a.astype(np.float32))
    return tuple(as32(a) for a in (left, left_t, right_w, right_t, back, final))


def per_device(micrograph, templates, defocus_values, defocus_group):
    tile_rows, tile_width = micrograph.shape
    margin = TPL // 2
    n = tile_width + 2 * margin
    h = n // 2 + 1
    tile_count = lax.axis_size("tile")
    pixel_count = float(tile_rows * tile_width * tile_count)
    local_sums = (jnp.sum(micrograph), jnp.sum(micrograph * micrograph))
    totals = lax.psum((local_sums[0], local_sums[1]), "tile")
    centre = totals[0] / pixel_count
    spread = jnp.sqrt(totals[1] / pixel_count - centre * centre + 1e-05)
    rows_ext = padded((micrograph - centre) / spread, (("tile", 0),), margin)

    gathered = lax.all_gather(templates, "tile", axis=1, tiled=True)[0]
    extent = gathered.shape[0]
    left, left_t, right_w, right_t, back, final = tables(tile_width, margin, extent)

    centred = gathered - jnp.mean(gathered)
    root_mean = jnp.sqrt(jnp.mean(centred * centred) + 1e-06)
    normed = centred / (root_mean * TPL)

    stage = product(left, rows_ext)
    spec = product(stage, right_w)
    a_c, a_s = spec[:h, :n], spec[:h, n:]
    b_c, b_s = spec[h:, :n], spec[h:, n:]
    spec_real = a_c - b_s
    spec_imag = -(a_s + b_c)

    stage_t = product(left_t, normed)
    spec_t = product(stage_t, right_t)
    ta_c, ta_s = spec_t[:h, :n], spec_t[:h, n:]
    tb_c, tb_s = spec_t[h:, :n], spec_t[h:, n:]
    template_real = ta_c - tb_s
    template_imag = -(ta_s + tb_c)

    positions = lax.iota(jnp.int32, n)
    signed_freq = (
        jnp.where(positions < n // 2, positions, positions - n).astype(jnp.float32) / n
    )
    freq_square = signed_freq[:h, None] ** 2 + signed_freq[None, :] ** 2
    group_ids = lax.iota(jnp.int32, defocus_values.shape[0])
    defocus = jnp.sum(jnp.where(group_ids == defocus_group[0], defocus_values, 0.0))
    phase_shift = math.pi * WAVELENGTH * defocus * freq_square
    contrast = -(
        math.sqrt(1.0 - AMPLITUDE * AMPLITUDE) * jnp.sin(phase_shift)
        + AMPLITUDE * jnp.cos(phase_shift)
    )
    product_real = (spec_real * template_real + spec_imag * template_imag) * contrast
    product_imag = (spec_imag * template_real - spec_real * template_imag) * contrast

    inner = product(jnp.concatenate([product_real, product_imag], axis=0), back)
    pr_c, pr_s = inner[:h, :tile_width], inner[:h, tile_width:]
    pi_c, pi_s = inner[h:, :tile_width], inner[h:, tile_width:]
    back_real = pr_c - pi_s
    back_imag = pr_s + pi_c
    scores = product(final, jnp.concatenate([back_real, back_imag[1:h - 1]], axis=0))

    orient_count = lax.axis_size("orient")
    share_rows = tile_rows // orient_count
    pieces = lax.all_to_all(scores, "orient", 0, 0, tiled=True).reshape(
        orient_count, share_rows, tile_width
    )
    top = pieces[0]
    second = jnp.full_like(top, -jnp.inf)
    total = pieces[0]
    squares = pieces[0] * pieces[0]
    for k in range(1, orient_count):
        value = pieces[k]
        second = jnp.maximum(second, jnp.minimum(top, value))
        top = jnp.maximum(top, value)
        total = total + value
        squares = squares + value * value
    mean_map = total / orient_count
    variance = squares / orient_count - mean_map * mean_map
    return (top, second, mean_map, variance)


def solution(mesh):
    placed = (P("tile", None), P("orient", "tile", None), P(), P("tile"))
    return jax.shard_map(
        per_device,
        mesh=mesh,
        in_specs=placed,
        out_specs=(
            P(("tile", "orient"), None),
            P(("tile", "orient"), None),
            P(("tile", "orient"), None),
            P(("tile", "orient"), None),
        ),
        check_vma=False,
    )
```

```python
import math

import numpy as np
import jax
import jax.numpy as jnp
from jax import lax
from jax.sharding import Mesh, PartitionSpec as P

TPL = 256


WAVELENGTH = 0.0197
AMPLITUDE = 0.07
mode = lax.Precision.HIGH


def padded(shard, sides, width):
    for axis, dim in sides:
        size, length = (lax.axis_size(axis), shard.shape[dim])
        up = [(i, (i + 1) % size) for i in range(size - 1)]
        down = [(j, i) for i, j in up]
        last = lax.slice_in_dim(shard, length - width, length, axis=dim)
        initial = lax.slice_in_dim(shard, 0, width, axis=dim)
        before = lax.ppermute(last, axis, up)
        after = lax.ppermute(initial, axis, down)
        shard = jnp.concatenate([before, shard, after], axis=dim)
    return shard


def product(former, latter):
    return jnp.dot(former, latter, precision=mode, preferred_element_type=jnp.float32)


def tables(tile_width, margin, extent):
    n = tile_width + 2 * margin
    h = n // 2 + 1
    idx = np.arange(n)
    angles = 2.0 * np.pi * ((idx[:, None] * idx[None, :]) % n) / n
    cos, sin = np.cos(angles), np.sin(angles)
    left = np.concatenate([cos[:h], sin[:h]], axis=0)
    left_t = left[:, :extent]
    right_w = np.concatenate([cos[margin:margin + tile_width], sin[margin:margin + tile_width]], axis=1)
    right_t = np.concatenate([cos[:extent], sin[:extent]], axis=1)
    back = np.concatenate([cos[:, :tile_width], sin[:, :tile_width]], axis=1)
    weight = np.full(h, 2.0)
    weight[0] = 1.0
    weight[-1] = 1.0
    final = np.concatenate(
        [cos[:tile_width, :h] * weight, -2.0 * sin[:tile_width, 1:h - 1]], axis=1
    ) / (n * n)
    as32 = lambda a: jnp.asarray(a.astype(np.float32))
    return tuple(as32(a) for a in (left, left_t, right_w, right_t, back, final))


def per_device(micrograph, templates, defocus_values, defocus_group):
    tile_rows, tile_width = micrograph.shape
    margin = TPL // 2
    n = tile_width + 2 * margin
    h = n // 2 + 1
    tile_count = lax.axis_size("tile")
    pixel_count = float(tile_rows * tile_width * tile_count)
    own_rows, tpl_width = templates.shape[1], templates.shape[2]
    sums = jnp.stack([jnp.sum(micrograph), jnp.sum(micrograph * micrograph)])
    payload = jnp.concatenate(
        [templates[0], jnp.pad(sums, (0, tpl_width - 2))[None]], axis=0
    )
    everything = lax.all_gather(payload, "tile")
    totals = jnp.sum(everything[:, own_rows, :2], axis=0)
    gathered = everything[:, :own_rows].reshape(tile_count * own_rows, tpl_width)
    centre = totals[0] / pixel_count
    spread = jnp.sqrt(totals[1] / pixel_count - centre * centre + 1e-05)
    rows_ext = padded((micrograph - centre) / spread, (("tile", 0),), margin)
    extent = gathered.shape[0]
    left, left_t, right_w, right_t, back, final = tables(tile_width, margin, extent)

    centred = gathered - jnp.mean(gathered)
    root_mean = jnp.sqrt(jnp.mean(centred * centred) + 1e-06)
    normed = centred / (root_mean * TPL)

    stage = product(left, rows_ext)
    spec = product(stage, right_w)
    a_c, a_s = spec[:h, :n], spec[:h, n:]
    b_c, b_s = spec[h:, :n], spec[h:, n:]
    spec_real = a_c - b_s
    spec_imag = -(a_s + b_c)

    stage_t = product(left_t, normed)
    spec_t = product(stage_t, right_t)
    ta_c, ta_s = spec_t[:h, :n], spec_t[:h, n:]
    tb_c, tb_s = spec_t[h:, :n], spec_t[h:, n:]
    template_real = ta_c - tb_s
    template_imag = -(ta_s + tb_c)

    positions = lax.iota(jnp.int32, n)
    signed_freq = (
        jnp.where(positions < n // 2, positions, positions - n).astype(jnp.float32) / n
    )
    freq_square = signed_freq[:h, None] ** 2 + signed_freq[None, :] ** 2
    group_ids = lax.iota(jnp.int32, defocus_values.shape[0])
    defocus = jnp.sum(jnp.where(group_ids == defocus_group[0], defocus_values, 0.0))
    phase_shift = math.pi * WAVELENGTH * defocus * freq_square
    contrast = -(
        math.sqrt(1.0 - AMPLITUDE * AMPLITUDE) * jnp.sin(phase_shift)
        + AMPLITUDE * jnp.cos(phase_shift)
    )
    product_real = (spec_real * template_real + spec_imag * template_imag) * contrast
    product_imag = (spec_imag * template_real - spec_real * template_imag) * contrast

    inner = product(jnp.concatenate([product_real, product_imag], axis=0), back)
    pr_c, pr_s = inner[:h, :tile_width], inner[:h, tile_width:]
    pi_c, pi_s = inner[h:, :tile_width], inner[h:, tile_width:]
    back_real = pr_c - pi_s
    back_imag = pr_s + pi_c
    scores = product(final, jnp.concatenate([back_real, back_imag[1:h - 1]], axis=0))

    outer, inner_count = lax.axis_size("oz"), lax.axis_size("oy")
    orient_count = outer * inner_count
    block = tile_rows // outer
    share_rows = block // inner_count
    pieces = lax.all_to_all(scores, "oz", 0, 0, tiled=True).reshape(outer, block, tile_width)
    top = pieces[0]
    second = jnp.full_like(top, -jnp.inf)
    total = pieces[0]
    squares = pieces[0] * pieces[0]
    for k in range(1, outer):
        value = pieces[k]
        second = jnp.maximum(second, jnp.minimum(top, value))
        top = jnp.maximum(top, value)
        total = total + value
        squares = squares + value * value
    partial = jnp.stack([top, second, total, squares], axis=0)
    partial = partial.reshape(4, inner_count, share_rows, tile_width).transpose(1, 0, 2, 3)
    parts = lax.all_to_all(
        partial.reshape(inner_count * 4, share_rows, tile_width), "oy", 0, 0, tiled=True
    ).reshape(inner_count, 4, share_rows, tile_width)
    top, second, total, squares = parts[0, 0], parts[0, 1], parts[0, 2], parts[0, 3]
    for k in range(1, inner_count):
        other_top, other_second = parts[k, 0], parts[k, 1]
        second = jnp.maximum(
            jnp.minimum(top, other_top), jnp.maximum(second, other_second)
        )
        top = jnp.maximum(top, other_top)
        total = total + parts[k, 2]
        squares = squares + parts[k, 3]
    mean_map = total / orient_count
    variance = squares / orient_count - mean_map * mean_map
    return (top, second, mean_map, variance)


def solution(mesh):
    tile_size, orient_size = mesh.devices.shape
    outer = 4 if orient_size % 4 == 0 else 1
    split = Mesh(
        mesh.devices.reshape(tile_size, outer, orient_size // outer), ("tile", "oz", "oy")
    )
    rows = P(("tile", "oz", "oy"), None)
    placed = (P("tile", None), P(("oz", "oy"), "tile", None), P(), P("tile"))
    return jax.shard_map(
        per_device,
        mesh=split,
        in_specs=placed,
        out_specs=(rows, rows, rows, rows),
        check_vma=False,
    )
```

```python
import math

import numpy as np
import jax
import jax.numpy as jnp
from jax import lax
from jax.sharding import PartitionSpec as P

TPL = 256


WAVELENGTH = 0.0197
AMPLITUDE = 0.07
mode = lax.Precision.HIGH


def padded(shard, sides, width):
    for axis, dim in sides:
        size, length = (lax.axis_size(axis), shard.shape[dim])
        up = [(i, (i + 1) % size) for i in range(size - 1)]
        down = [(j, i) for i, j in up]
        last = lax.slice_in_dim(shard, length - width, length, axis=dim)
        initial = lax.slice_in_dim(shard, 0, width, axis=dim)
        before = lax.ppermute(last, axis, up)
        after = lax.ppermute(initial, axis, down)
        shard = jnp.concatenate([before, shard, after], axis=dim)
    return shard


def product(former, latter):
    return jnp.dot(former, latter, precision=mode, preferred_element_type=jnp.float32)


def tables(tile_width, margin, extent):
    n = tile_width + 2 * margin
    h = n // 2 + 1
    idx = np.arange(n)
    angles = 2.0 * np.pi * ((idx[:, None] * idx[None, :]) % n) / n
    cos, sin = np.cos(angles), np.sin(angles)
    left = np.concatenate([cos[:h], sin[:h]], axis=0)
    left_t = left[:, :extent]
    right_w = np.concatenate([cos[margin:margin + tile_width], sin[margin:margin + tile_width]], axis=1)
    right_t = np.concatenate([cos[:extent], sin[:extent]], axis=1)
    back = np.concatenate([cos[:, :tile_width], sin[:, :tile_width]], axis=1)
    weight = np.full(h, 2.0)
    weight[0] = 1.0
    weight[-1] = 1.0
    final = np.concatenate(
        [cos[:tile_width, :h] * weight, -2.0 * sin[:tile_width, 1:h - 1]], axis=1
    ) / (n * n)
    as32 = lambda a: jnp.asarray(a.astype(np.float32))
    return tuple(as32(a) for a in (left, left_t, right_w, right_t, back, final))


def per_device(micrograph, templates, defocus_values, defocus_group):
    tile_rows, tile_width = micrograph.shape
    margin = TPL // 2
    n = tile_width + 2 * margin
    h = n // 2 + 1
    tile_count = lax.axis_size("tile")
    pixel_count = float(tile_rows * tile_width * tile_count)
    own_rows, tpl_width = templates.shape[1], templates.shape[2]
    halo = padded(micrograph, (("tile", 0),), margin)
    sums = jnp.stack([jnp.sum(micrograph), jnp.sum(micrograph * micrograph)])
    payload = jnp.concatenate(
        [templates[0], jnp.pad(sums, (0, tpl_width - 2))[None]], axis=0
    )
    everything = lax.all_gather(payload, "tile")
    totals = jnp.sum(everything[:, own_rows, :2], axis=0)
    gathered = everything[:, :own_rows].reshape(tile_count * own_rows, tpl_width)
    centre = totals[0] / pixel_count
    spread = jnp.sqrt(totals[1] / pixel_count - centre * centre + 1e-05)
    tile_index = lax.axis_index("tile")
    row_ids = lax.broadcasted_iota(jnp.int32, (n, 1), 0)
    valid = ((row_ids >= margin) | (tile_index > 0)) & (
        (row_ids < margin + tile_rows) | (tile_index < tile_count - 1)
    )
    rows_ext = lax.optimization_barrier(jnp.where(valid, (halo - centre) / spread, 0.0))
    extent = gathered.shape[0]
    left, left_t, right_w, right_t, back, final = tables(tile_width, margin, extent)

    centred = gathered - jnp.mean(gathered)
    root_mean = jnp.sqrt(jnp.mean(centred * centred) + 1e-06)
    normed = centred / (root_mean * TPL)

    stage = product(left, rows_ext)
    spec = product(stage, right_w)
    a_c, a_s = spec[:h, :n], spec[:h, n:]
    b_c, b_s = spec[h:, :n], spec[h:, n:]
    spec_real = a_c - b_s
    spec_imag = -(a_s + b_c)

    stage_t = product(left_t, normed)
    spec_t = product(stage_t, right_t)
    ta_c, ta_s = spec_t[:h, :n], spec_t[:h, n:]
    tb_c, tb_s = spec_t[h:, :n], spec_t[h:, n:]
    template_real = ta_c - tb_s
    template_imag = -(ta_s + tb_c)

    positions = lax.iota(jnp.int32, n)
    signed_freq = (
        jnp.where(positions < n // 2, positions, positions - n).astype(jnp.float32) / n
    )
    group_ids = lax.iota(jnp.int32, defocus_values.shape[0])
    defocus = jnp.sum(jnp.where(group_ids == defocus_group[0], defocus_values, 0.0))
    scale = math.pi * WAVELENGTH * defocus
    row_phase = scale * signed_freq[:h, None] ** 2
    col_phase = scale * signed_freq[None, :] ** 2
    sin_r, cos_r = jnp.sin(row_phase), jnp.cos(row_phase)
    sin_c, cos_c = jnp.sin(col_phase), jnp.cos(col_phase)
    weight_sin = math.sqrt(1.0 - AMPLITUDE * AMPLITUDE)
    col_u = weight_sin * cos_c - AMPLITUDE * sin_c
    col_v = weight_sin * sin_c + AMPLITUDE * cos_c
    contrast = -(sin_r * col_u + cos_r * col_v)
    product_real = (spec_real * template_real + spec_imag * template_imag) * contrast
    product_imag = (spec_imag * template_real - spec_real * template_imag) * contrast

    inner = product(jnp.concatenate([product_real, product_imag], axis=0), back)
    pr_c, pr_s = inner[:h, :tile_width], inner[:h, tile_width:]
    pi_c, pi_s = inner[h:, :tile_width], inner[h:, tile_width:]
    back_real = pr_c - pi_s
    back_imag = pr_s + pi_c
    scores = product(final, jnp.concatenate([back_real, back_imag[1:h - 1]], axis=0))

    orient_count = lax.axis_size("orient")
    share_rows = tile_rows // orient_count
    pieces = lax.all_to_all(scores, "orient", 0, 0, tiled=True).reshape(
        orient_count, share_rows, tile_width
    )
    top = pieces[0]
    second = jnp.full_like(top, -jnp.inf)
    total = pieces[0]
    squares = pieces[0] * pieces[0]
    for k in range(1, orient_count):
        value = pieces[k]
        second = jnp.maximum(second, jnp.minimum(top, value))
        top = jnp.maximum(top, value)
        total = total + value
        squares = squares + value * value
    mean_map = total / orient_count
    variance = squares / orient_count - mean_map * mean_map
    return (top, second, mean_map, variance)


def solution(mesh):
    placed = (P("tile", None), P("orient", "tile", None), P(), P("tile"))
    return jax.shard_map(
        per_device,
        mesh=mesh,
        in_specs=placed,
        out_specs=(
            P(("tile", "orient"), None),
            P(("tile", "orient"), None),
            P(("tile", "orient"), None),
            P(("tile", "orient"), None),
        ),
        check_vma=False,
    )
```

```python
import math

import numpy as np
import jax
import jax.numpy as jnp
from jax import lax
from jax.sharding import PartitionSpec as P

TPL = 256


WAVELENGTH = 0.0197
AMPLITUDE = 0.07
mode = lax.Precision.HIGH


def padded(shard, sides, width):
    for axis, dim in sides:
        size, length = (lax.axis_size(axis), shard.shape[dim])
        up = [(i, (i + 1) % size) for i in range(size - 1)]
        down = [(j, i) for i, j in up]
        last = lax.slice_in_dim(shard, length - width, length, axis=dim)
        initial = lax.slice_in_dim(shard, 0, width, axis=dim)
        before = lax.ppermute(last, axis, up)
        after = lax.ppermute(initial, axis, down)
        shard = jnp.concatenate([before, shard, after], axis=dim)
    return shard


def product(former, latter):
    return jnp.dot(former, latter, precision=mode, preferred_element_type=jnp.float32)


def tables(tile_width, margin, extent):
    n = tile_width + 2 * margin
    h = n // 2 + 1
    idx = np.arange(n)
    angles = 2.0 * np.pi * ((idx[:, None] * idx[None, :]) % n) / n
    cos, sin = np.cos(angles), np.sin(angles)
    left = np.concatenate([cos[:h], sin[1:h - 1]], axis=0)
    left_t = left[:, :extent]
    right_w = np.concatenate([cos[margin:margin + tile_width], sin[margin:margin + tile_width]], axis=1)
    right_t = np.concatenate([cos[:extent], sin[:extent]], axis=1)
    back = np.concatenate([cos[:, :tile_width], sin[:, :tile_width]], axis=1)
    weight = np.full(h, 2.0)
    weight[0] = 1.0
    weight[-1] = 1.0
    final = np.concatenate(
        [cos[:tile_width, :h] * weight, -2.0 * sin[:tile_width, 1:h - 1]], axis=1
    ) / (n * n)
    as32 = lambda a: jnp.asarray(a.astype(np.float32))
    return tuple(as32(a) for a in (left, left_t, right_w, right_t, back, final))


def per_device(micrograph, templates, defocus_values, defocus_group):
    tile_rows, tile_width = micrograph.shape
    margin = TPL // 2
    n = tile_width + 2 * margin
    h = n // 2 + 1
    tile_count = lax.axis_size("tile")
    pixel_count = float(tile_rows * tile_width * tile_count)
    own_rows, tpl_width = templates.shape[1], templates.shape[2]
    halo = padded(micrograph, (("tile", 0),), margin)
    sums = jnp.stack([jnp.sum(micrograph), jnp.sum(micrograph * micrograph)])
    payload = jnp.concatenate(
        [templates[0], jnp.pad(sums, (0, tpl_width - 2))[None]], axis=0
    )
    everything = lax.all_gather(payload, "tile")
    totals = jnp.sum(everything[:, own_rows, :2], axis=0)
    gathered = everything[:, :own_rows].reshape(tile_count * own_rows, tpl_width)
    centre = totals[0] / pixel_count
    spread = jnp.sqrt(totals[1] / pixel_count - centre * centre + 1e-05)
    tile_index = lax.axis_index("tile")
    row_ids = lax.broadcasted_iota(jnp.int32, (n, 1), 0)
    valid = ((row_ids >= margin) | (tile_index > 0)) & (
        (row_ids < margin + tile_rows) | (tile_index < tile_count - 1)
    )
    rows_ext = lax.optimization_barrier(jnp.where(valid, (halo - centre) / spread, 0.0))
    extent = gathered.shape[0]
    left, left_t, right_w, right_t, back, final = tables(tile_width, margin, extent)

    centred = gathered - jnp.mean(gathered)
    root_mean = jnp.sqrt(jnp.mean(centred * centred) + 1e-06)
    normed = centred / (root_mean * TPL)

    stage = product(left, rows_ext)
    spec = product(stage, right_w)
    edge = ((1, 1), (0, 0))
    a_c, a_s = spec[:h, :n], spec[:h, n:]
    b_c, b_s = jnp.pad(spec[h:, :n], edge), jnp.pad(spec[h:, n:], edge)
    spec_real = a_c - b_s
    spec_imag = -(a_s + b_c)

    stage_t = product(left_t, normed)
    spec_t = product(stage_t, right_t)
    ta_c, ta_s = spec_t[:h, :n], spec_t[:h, n:]
    tb_c, tb_s = jnp.pad(spec_t[h:, :n], edge), jnp.pad(spec_t[h:, n:], edge)
    template_real = ta_c - tb_s
    template_imag = -(ta_s + tb_c)

    positions = lax.iota(jnp.int32, n)
    signed_freq = (
        jnp.where(positions < n // 2, positions, positions - n).astype(jnp.float32) / n
    )
    group_ids = lax.iota(jnp.int32, defocus_values.shape[0])
    defocus = jnp.sum(jnp.where(group_ids == defocus_group[0], defocus_values, 0.0))
    scale = math.pi * WAVELENGTH * defocus
    row_phase = scale * signed_freq[:h, None] ** 2
    col_phase = scale * signed_freq[None, :] ** 2
    sin_r, cos_r = jnp.sin(row_phase), jnp.cos(row_phase)
    sin_c, cos_c = jnp.sin(col_phase), jnp.cos(col_phase)
    weight_sin = math.sqrt(1.0 - AMPLITUDE * AMPLITUDE)
    col_u = weight_sin * cos_c - AMPLITUDE * sin_c
    col_v = weight_sin * sin_c + AMPLITUDE * cos_c
    contrast = -(sin_r * col_u + cos_r * col_v)
    product_real = (spec_real * template_real + spec_imag * template_imag) * contrast
    product_imag = (spec_imag * template_real - spec_real * template_imag) * contrast

    inner = product(jnp.concatenate([product_real, product_imag], axis=0), back)
    pr_c, pr_s = inner[:h, :tile_width], inner[:h, tile_width:]
    pi_c, pi_s = inner[h:, :tile_width], inner[h:, tile_width:]
    back_real = pr_c - pi_s
    back_imag = pr_s + pi_c
    scores = product(final, jnp.concatenate([back_real, back_imag[1:h - 1]], axis=0))

    orient_count = lax.axis_size("orient")
    share_rows = tile_rows // orient_count
    pieces = lax.all_to_all(scores, "orient", 0, 0, tiled=True).reshape(
        orient_count, share_rows, tile_width
    )
    top = pieces[0]
    second = jnp.full_like(top, -jnp.inf)
    total = pieces[0]
    squares = pieces[0] * pieces[0]
    for k in range(1, orient_count):
        value = pieces[k]
        second = jnp.maximum(second, jnp.minimum(top, value))
        top = jnp.maximum(top, value)
        total = total + value
        squares = squares + value * value
    mean_map = total / orient_count
    variance = squares / orient_count - mean_map * mean_map
    return (top, second, mean_map, variance)


def solution(mesh):
    placed = (P("tile", None), P("orient", "tile", None), P(), P("tile"))
    return jax.shard_map(
        per_device,
        mesh=mesh,
        in_specs=placed,
        out_specs=(
            P(("tile", "orient"), None),
            P(("tile", "orient"), None),
            P(("tile", "orient"), None),
            P(("tile", "orient"), None),
        ),
        check_vma=False,
    )
```

```python
import math

import numpy as np
import jax
import jax.numpy as jnp
from jax import lax
from jax.sharding import PartitionSpec as P

TPL = 256


WAVELENGTH = 0.0197
AMPLITUDE = 0.07
mode = lax.Precision.HIGH


def padded(shard, sides, width):
    for axis, dim in sides:
        size, length = (lax.axis_size(axis), shard.shape[dim])
        up = [(i, (i + 1) % size) for i in range(size - 1)]
        down = [(j, i) for i, j in up]
        last = lax.slice_in_dim(shard, length - width, length, axis=dim)
        initial = lax.slice_in_dim(shard, 0, width, axis=dim)
        before = lax.ppermute(last, axis, up)
        after = lax.ppermute(initial, axis, down)
        shard = jnp.concatenate([before, shard, after], axis=dim)
    return shard


def product(former, latter):
    return jnp.dot(former, latter, precision=mode, preferred_element_type=jnp.float32)


def tables(tile_width, margin, extent):
    n = tile_width + 2 * margin
    h = n // 2 + 1
    idx = np.arange(n)
    angles = 2.0 * np.pi * ((idx[:, None] * idx[None, :]) % n) / n
    cos, sin = np.cos(angles), np.sin(angles)
    left = np.concatenate([cos[:h], sin[1:h - 1]], axis=0)
    left_t = left[:, :extent]
    right_w = np.concatenate([cos[margin:margin + tile_width], sin[margin:margin + tile_width]], axis=1)
    right_t = np.concatenate([cos[:extent], sin[:extent]], axis=1)
    back = np.concatenate([cos[:, :tile_width], sin[:, :tile_width]], axis=1)
    weight = np.full(h, 2.0)
    weight[0] = 1.0
    weight[-1] = 1.0
    final = np.concatenate(
        [cos[:tile_width, :h] * weight, -2.0 * sin[:tile_width, 1:h - 1]], axis=1
    ) / (n * n)
    as32 = lambda a: jnp.asarray(a.astype(np.float32))
    return tuple(as32(a) for a in (left, left_t, right_w, right_t, back, final))


def per_device(micrograph, templates, defocus_values, defocus_group):
    tile_rows, tile_width = micrograph.shape
    margin = TPL // 2
    n = tile_width + 2 * margin
    h = n // 2 + 1
    tile_count = lax.axis_size("tile")
    pixel_count = float(tile_rows * tile_width * tile_count)
    own_rows, tpl_width = templates.shape[1], templates.shape[2]
    halo = padded(micrograph, (("tile", 0),), margin)
    own_tpl = templates[0]
    own_count = float(own_rows * tpl_width)
    own_mean = jnp.sum(own_tpl) / own_count
    own_spread = jnp.sum((own_tpl - own_mean) ** 2)
    lane = lax.broadcasted_iota(jnp.int32, (1, tpl_width), 1)
    stats_row = jnp.where(lane == 0, jnp.sum(micrograph), 0.0)
    stats_row = jnp.where(lane == 1, jnp.sum(micrograph * micrograph), stats_row)
    stats_row = jnp.where(lane == 2, own_mean, stats_row)
    stats_row = jnp.where(lane == 3, own_spread, stats_row)
    payload = jnp.concatenate([own_tpl, stats_row], axis=0)
    everything = lax.all_gather(payload, "tile")
    totals = jnp.sum(everything[:, own_rows, :2], axis=0)
    gathered = everything[:, :own_rows].reshape(tile_count * own_rows, tpl_width)
    centre = totals[0] / pixel_count
    spread = jnp.sqrt(totals[1] / pixel_count - centre * centre + 1e-05)
    part_means = everything[:, own_rows, 2]
    tpl_mean = jnp.mean(part_means)
    tpl_m2 = jnp.sum(everything[:, own_rows, 3]) + own_count * jnp.sum(
        (part_means - tpl_mean) ** 2
    )
    root_mean = jnp.sqrt(tpl_m2 / (own_count * tile_count) + 1e-06)
    tile_index = lax.axis_index("tile")
    row_ids = lax.broadcasted_iota(jnp.int32, (n, 1), 0)
    valid = ((row_ids >= margin) | (tile_index > 0)) & (
        (row_ids < margin + tile_rows) | (tile_index < tile_count - 1)
    )
    rows_ext = lax.optimization_barrier(jnp.where(valid, (halo - centre) / spread, 0.0))
    extent = gathered.shape[0]
    left, left_t, right_w, right_t, back, final = tables(tile_width, margin, extent)

    normed = (gathered - tpl_mean) / (root_mean * TPL)

    stage = product(left, rows_ext)
    spec = product(stage, right_w)
    edge = ((1, 1), (0, 0))
    a_c, a_s = spec[:h, :n], spec[:h, n:]
    b_c, b_s = jnp.pad(spec[h:, :n], edge), jnp.pad(spec[h:, n:], edge)
    spec_real = a_c - b_s
    spec_imag = -(a_s + b_c)

    stage_t = product(left_t, normed)
    spec_t = product(stage_t, right_t)
    ta_c, ta_s = spec_t[:h, :n], spec_t[:h, n:]
    tb_c, tb_s = jnp.pad(spec_t[h:, :n], edge), jnp.pad(spec_t[h:, n:], edge)
    template_real = ta_c - tb_s
    template_imag = -(ta_s + tb_c)

    positions = lax.iota(jnp.int32, n)
    signed_freq = (
        jnp.where(positions < n // 2, positions, positions - n).astype(jnp.float32) / n
    )
    group_ids = lax.iota(jnp.int32, defocus_values.shape[0])
    defocus = jnp.sum(jnp.where(group_ids == defocus_group[0], defocus_values, 0.0))
    scale = math.pi * WAVELENGTH * defocus
    row_phase = scale * signed_freq[:h, None] ** 2
    col_phase = scale * signed_freq[None, :] ** 2
    sin_r, cos_r = jnp.sin(row_phase), jnp.cos(row_phase)
    sin_c, cos_c = jnp.sin(col_phase), jnp.cos(col_phase)
    weight_sin = math.sqrt(1.0 - AMPLITUDE * AMPLITUDE)
    col_u = weight_sin * cos_c - AMPLITUDE * sin_c
    col_v = weight_sin * sin_c + AMPLITUDE * cos_c
    contrast = -(sin_r * col_u + cos_r * col_v)
    product_real = (spec_real * template_real + spec_imag * template_imag) * contrast
    product_imag = (spec_imag * template_real - spec_real * template_imag) * contrast

    inner = product(jnp.concatenate([product_real, product_imag], axis=0), back)
    pr_c, pr_s = inner[:h, :tile_width], inner[:h, tile_width:]
    pi_c, pi_s = inner[h:, :tile_width], inner[h:, tile_width:]
    back_real = pr_c - pi_s
    back_imag = pr_s + pi_c
    scores = product(final, jnp.concatenate([back_real, back_imag[1:h - 1]], axis=0))

    orient_count = lax.axis_size("orient")
    share_rows = tile_rows // orient_count
    pieces = lax.all_to_all(scores, "orient", 0, 0, tiled=True).reshape(
        orient_count, share_rows, tile_width
    )
    top = pieces[0]
    second = jnp.full_like(top, -jnp.inf)
    total = pieces[0]
    squares = pieces[0] * pieces[0]
    for k in range(1, orient_count):
        value = pieces[k]
        second = jnp.maximum(second, jnp.minimum(top, value))
        top = jnp.maximum(top, value)
        total = total + value
        squares = squares + value * value
    mean_map = total / orient_count
    variance = squares / orient_count - mean_map * mean_map
    return (top, second, mean_map, variance)


def solution(mesh):
    placed = (P("tile", None), P("orient", "tile", None), P(), P("tile"))
    return jax.shard_map(
        per_device,
        mesh=mesh,
        in_specs=placed,
        out_specs=(
            P(("tile", "orient"), None),
            P(("tile", "orient"), None),
            P(("tile", "orient"), None),
            P(("tile", "orient"), None),
        ),
        check_vma=False,
    )
```

```python
import math

import numpy as np
import jax
import jax.numpy as jnp
from jax import lax
from jax.sharding import PartitionSpec as P

TPL = 256


WAVELENGTH = 0.0197
AMPLITUDE = 0.07
mode = lax.Precision.HIGH


def padded(shard, sides, width):
    for axis, dim in sides:
        size, length = (lax.axis_size(axis), shard.shape[dim])
        up = [(i, (i + 1) % size) for i in range(size - 1)]
        down = [(j, i) for i, j in up]
        last = lax.slice_in_dim(shard, length - width, length, axis=dim)
        initial = lax.slice_in_dim(shard, 0, width, axis=dim)
        before = lax.ppermute(last, axis, up)
        after = lax.ppermute(initial, axis, down)
        shard = jnp.concatenate([before, shard, after], axis=dim)
    return shard


def product(former, latter):
    return jnp.dot(former, latter, precision=mode, preferred_element_type=jnp.float32)


def tables(tile_width, margin, extent):
    n = tile_width + 2 * margin
    h = n // 2 + 1
    idx = np.arange(n)
    angles = 2.0 * np.pi * ((idx[:, None] * idx[None, :]) % n) / n
    cos, sin = np.cos(angles), np.sin(angles)
    left = np.concatenate([cos[:h], sin[1:h - 1]], axis=0)
    left_t = left[:, :extent]
    window_cols = slice(margin, margin + tile_width)
    right_w = np.concatenate([cos[window_cols, :h], sin[window_cols, 1:h - 1]], axis=1)
    right_t = np.concatenate([cos[:extent, :h], sin[:extent, 1:h - 1]], axis=1)
    mirror = np.concatenate([np.arange(h), n - np.arange(1, h - 1)])
    back = np.concatenate([cos[mirror, :tile_width], sin[mirror, :tile_width]], axis=1)
    weight = np.full(h, 2.0)
    weight[0] = 1.0
    weight[-1] = 1.0
    final = np.concatenate(
        [cos[:tile_width, :h] * weight, -2.0 * sin[:tile_width, 1:h - 1]], axis=1
    ) / (n * n)
    as32 = lambda a: jnp.asarray(a.astype(np.float32))
    return tuple(as32(a) for a in (left, left_t, right_w, right_t, back, final))


def per_device(micrograph, templates, defocus_values, defocus_group):
    tile_rows, tile_width = micrograph.shape
    margin = TPL // 2
    n = tile_width + 2 * margin
    h = n // 2 + 1
    tile_count = lax.axis_size("tile")
    pixel_count = float(tile_rows * tile_width * tile_count)
    own_rows, tpl_width = templates.shape[1], templates.shape[2]
    halo = padded(micrograph, (("tile", 0),), margin)
    sums = jnp.stack([jnp.sum(micrograph), jnp.sum(micrograph * micrograph)])
    payload = jnp.concatenate(
        [templates[0], jnp.pad(sums, (0, tpl_width - 2))[None]], axis=0
    )
    everything = lax.all_gather(payload, "tile")
    totals = jnp.sum(everything[:, own_rows, :2], axis=0)
    gathered = everything[:, :own_rows].reshape(tile_count * own_rows, tpl_width)
    centre = totals[0] / pixel_count
    spread = jnp.sqrt(totals[1] / pixel_count - centre * centre + 1e-05)
    tile_index = lax.axis_index("tile")
    row_ids = lax.broadcasted_iota(jnp.int32, (n, 1), 0)
    valid = ((row_ids >= margin) | (tile_index > 0)) & (
        (row_ids < margin + tile_rows) | (tile_index < tile_count - 1)
    )
    rows_ext = lax.optimization_barrier(jnp.where(valid, (halo - centre) / spread, 0.0))
    extent = gathered.shape[0]
    left, left_t, right_w, right_t, back, final = tables(tile_width, margin, extent)

    centred = gathered - jnp.mean(gathered)
    root_mean = jnp.sqrt(jnp.mean(centred * centred) + 1e-06)
    normed = centred / (root_mean * TPL)

    def spectrum(packed):
        edge_rows, edge_cols = ((1, 1), (0, 0)), ((0, 0), (1, 1))
        ga, gb = packed[:h], jnp.pad(packed[h:], edge_rows)
        ga_s = jnp.pad(ga[:, h:], edge_cols)
        gb_s = jnp.pad(gb[:, h:], edge_cols)
        real = jnp.concatenate([ga[:, :h] - gb_s, ga[:, 1:h - 1] + gb[:, h:]], axis=1)
        imag = jnp.concatenate([-(ga_s + gb[:, :h]), ga[:, h:] - gb[:, 1:h - 1]], axis=1)
        return real, imag

    spec_real, spec_imag = spectrum(product(product(left, rows_ext), right_w))
    template_real, template_imag = spectrum(product(product(left_t, normed), right_t))

    positions = lax.iota(jnp.int32, n)
    signed_freq = (
        jnp.where(positions < n // 2, positions, positions - n).astype(jnp.float32) / n
    )
    packed_freq = jnp.where(positions < h, positions, positions - (h - 1)).astype(jnp.float32) / n
    group_ids = lax.iota(jnp.int32, defocus_values.shape[0])
    defocus = jnp.sum(jnp.where(group_ids == defocus_group[0], defocus_values, 0.0))
    scale = math.pi * WAVELENGTH * defocus
    row_phase = scale * signed_freq[:h, None] ** 2
    col_phase = scale * packed_freq[None, :] ** 2
    sin_r, cos_r = jnp.sin(row_phase), jnp.cos(row_phase)
    sin_c, cos_c = jnp.sin(col_phase), jnp.cos(col_phase)
    weight_sin = math.sqrt(1.0 - AMPLITUDE * AMPLITUDE)
    col_u = weight_sin * cos_c - AMPLITUDE * sin_c
    col_v = weight_sin * sin_c + AMPLITUDE * cos_c
    contrast = -(sin_r * col_u + cos_r * col_v)
    product_real = (spec_real * template_real + spec_imag * template_imag) * contrast
    product_imag = (spec_imag * template_real - spec_real * template_imag) * contrast

    inner = product(jnp.concatenate([product_real, product_imag], axis=0), back)
    pr_c, pr_s = inner[:h, :tile_width], inner[:h, tile_width:]
    pi_c, pi_s = inner[h:, :tile_width], inner[h:, tile_width:]
    back_real = pr_c - pi_s
    back_imag = pr_s + pi_c
    scores = product(final, jnp.concatenate([back_real, back_imag[1:h - 1]], axis=0))

    orient_count = lax.axis_size("orient")
    share_rows = tile_rows // orient_count
    pieces = lax.all_to_all(scores, "orient", 0, 0, tiled=True).reshape(
        orient_count, share_rows, tile_width
    )
    top = pieces[0]
    second = jnp.full_like(top, -jnp.inf)
    total = pieces[0]
    squares = pieces[0] * pieces[0]
    for k in range(1, orient_count):
        value = pieces[k]
        second = jnp.maximum(second, jnp.minimum(top, value))
        top = jnp.maximum(top, value)
        total = total + value
        squares = squares + value * value
    mean_map = total / orient_count
    variance = squares / orient_count - mean_map * mean_map
    return (top, second, mean_map, variance)


def solution(mesh):
    placed = (P("tile", None), P("orient", "tile", None), P(), P("tile"))
    return jax.shard_map(
        per_device,
        mesh=mesh,
        in_specs=placed,
        out_specs=(
            P(("tile", "orient"), None),
            P(("tile", "orient"), None),
            P(("tile", "orient"), None),
            P(("tile", "orient"), None),
        ),
        check_vma=False,
    )
```

```python
import math

import numpy as np
import jax
import jax.numpy as jnp
from jax import lax
from jax.sharding import PartitionSpec as P

TPL = 256


WAVELENGTH = 0.0197
AMPLITUDE = 0.07
mode = lax.Precision.HIGH


def padded(shard, sides, width):
    for axis, dim in sides:
        size, length = (lax.axis_size(axis), shard.shape[dim])
        up = [(i, (i + 1) % size) for i in range(size - 1)]
        down = [(j, i) for i, j in up]
        last = lax.slice_in_dim(shard, length - width, length, axis=dim)
        initial = lax.slice_in_dim(shard, 0, width, axis=dim)
        before = lax.ppermute(last, axis, up)
        after = lax.ppermute(initial, axis, down)
        shard = jnp.concatenate([before, shard, after], axis=dim)
    return shard


def product(former, latter):
    return jnp.dot(former, latter, precision=mode, preferred_element_type=jnp.float32)


def tables(tile_width, margin, extent):
    n = tile_width + 2 * margin
    h = n // 2 + 1
    idx = np.arange(n)
    angles = 2.0 * np.pi * ((idx[:, None] * idx[None, :]) % n) / n
    cos, sin = np.cos(angles), np.sin(angles)
    left = np.concatenate([cos[:h], sin[1:h - 1]], axis=0)
    left_t = left[:, :extent]
    window_cols = slice(margin, margin + tile_width)
    right_w = np.concatenate([cos[window_cols, :h], sin[window_cols, 1:h - 1]], axis=1)
    right_t = np.concatenate([cos[:extent, :h], sin[:extent, 1:h - 1]], axis=1)
    mirror = np.concatenate([np.arange(h), n - np.arange(1, h - 1)])
    back = np.concatenate([cos[mirror, :tile_width], sin[mirror, :tile_width]], axis=1)
    weight = np.full(h, 2.0)
    weight[0] = 1.0
    weight[-1] = 1.0
    final = np.concatenate(
        [cos[:tile_width, :h] * weight, -2.0 * sin[:tile_width, 1:h - 1]], axis=1
    ) / (n * n)
    as32 = lambda a: jnp.asarray(a.astype(np.float32))
    return tuple(as32(a) for a in (left, left_t, right_w, right_t, back, final))


def per_device(micrograph, templates, defocus_values, defocus_group):
    tile_rows, tile_width = micrograph.shape
    margin = TPL // 2
    n = tile_width + 2 * margin
    h = n // 2 + 1
    tile_count = lax.axis_size("tile")
    pixel_count = float(tile_rows * tile_width * tile_count)
    own_rows, tpl_width = templates.shape[1], templates.shape[2]
    halo = padded(micrograph, (("tile", 0),), margin)
    sums = jnp.stack([jnp.sum(micrograph), jnp.sum(micrograph * micrograph)])
    payload = jnp.concatenate(
        [templates[0], jnp.pad(sums, (0, tpl_width - 2))[None]], axis=0
    )
    everything = lax.all_gather(payload, "tile")
    totals = jnp.sum(everything[:, own_rows, :2], axis=0)
    gathered = everything[:, :own_rows].reshape(tile_count * own_rows, tpl_width)
    centre = totals[0] / pixel_count
    spread = jnp.sqrt(totals[1] / pixel_count - centre * centre + 1e-05)
    tile_index = lax.axis_index("tile")
    row_ids = lax.broadcasted_iota(jnp.int32, (n, 1), 0)
    valid = ((row_ids >= margin) | (tile_index > 0)) & (
        (row_ids < margin + tile_rows) | (tile_index < tile_count - 1)
    )
    rows_ext = lax.optimization_barrier(jnp.where(valid, (halo - centre) / spread, 0.0))
    extent = gathered.shape[0]
    left, left_t, right_w, right_t, back, final = tables(tile_width, margin, extent)

    centred = gathered - jnp.mean(gathered)
    root_mean = jnp.sqrt(jnp.mean(centred * centred) + 1e-06)
    normed = centred / (root_mean * TPL)

    edge_rows, edge_cols = ((1, 1), (0, 0)), ((0, 0), (1, 1))

    def halves(packed):
        return packed[:h], jnp.pad(packed[h:], edge_rows)

    def direct(ga, gb):
        ga_s, gb_s = jnp.pad(ga[:, h:], edge_cols), jnp.pad(gb[:, h:], edge_cols)
        return ga[:, :h] - gb_s, -(ga_s + gb[:, :h])

    def mirrored(ga, gb):
        return ga[:, 1:h - 1] + gb[:, h:], ga[:, h:] - gb[:, 1:h - 1]

    window_parts = halves(product(product(left, rows_ext), right_w))
    template_parts = halves(product(product(left_t, normed), right_t))

    positions = lax.iota(jnp.int32, n)
    signed_freq = (
        jnp.where(positions < n // 2, positions, positions - n).astype(jnp.float32) / n
    )
    packed_freq = jnp.where(positions < h, positions, positions - (h - 1)).astype(jnp.float32) / n
    group_ids = lax.iota(jnp.int32, defocus_values.shape[0])
    defocus = jnp.sum(jnp.where(group_ids == defocus_group[0], defocus_values, 0.0))
    scale = math.pi * WAVELENGTH * defocus
    row_phase = scale * signed_freq[:h, None] ** 2
    col_phase = scale * packed_freq[None, :] ** 2
    sin_r, cos_r = jnp.sin(row_phase), jnp.cos(row_phase)
    sin_c, cos_c = jnp.sin(col_phase), jnp.cos(col_phase)
    weight_sin = math.sqrt(1.0 - AMPLITUDE * AMPLITUDE)
    col_u = weight_sin * cos_c - AMPLITUDE * sin_c
    col_v = weight_sin * sin_c + AMPLITUDE * cos_c
    contrast = -(sin_r * col_u + cos_r * col_v)
    def multiply(form, weight):
        spec_real, spec_imag = form(*window_parts)
        template_real, template_imag = form(*template_parts)
        return (
            (spec_real * template_real + spec_imag * template_imag) * weight,
            (spec_imag * template_real - spec_real * template_imag) * weight,
        )

    real_d, imag_d = multiply(direct, contrast[:, :h])
    real_m, imag_m = multiply(mirrored, contrast[:, h:])
    lhs = jnp.concatenate(
        [jnp.concatenate([real_d, real_m], axis=1), jnp.concatenate([imag_d, imag_m], axis=1)],
        axis=0,
    )
    inner = product(lhs, back)
    pr_c, pr_s = inner[:h, :tile_width], inner[:h, tile_width:]
    pi_c, pi_s = inner[h:, :tile_width], inner[h:, tile_width:]
    back_real = pr_c - pi_s
    back_imag = pr_s + pi_c
    scores = product(final, jnp.concatenate([back_real, back_imag[1:h - 1]], axis=0))

    orient_count = lax.axis_size("orient")
    share_rows = tile_rows // orient_count
    pieces = lax.all_to_all(scores, "orient", 0, 0, tiled=True).reshape(
        orient_count, share_rows, tile_width
    )
    top = pieces[0]
    second = jnp.full_like(top, -jnp.inf)
    total = pieces[0]
    squares = pieces[0] * pieces[0]
    for k in range(1, orient_count):
        value = pieces[k]
        second = jnp.maximum(second, jnp.minimum(top, value))
        top = jnp.maximum(top, value)
        total = total + value
        squares = squares + value * value
    mean_map = total / orient_count
    variance = squares / orient_count - mean_map * mean_map
    return (top, second, mean_map, variance)


def solution(mesh):
    placed = (P("tile", None), P("orient", "tile", None), P(), P("tile"))
    return jax.shard_map(
        per_device,
        mesh=mesh,
        in_specs=placed,
        out_specs=(
            P(("tile", "orient"), None),
            P(("tile", "orient"), None),
            P(("tile", "orient"), None),
            P(("tile", "orient"), None),
        ),
        check_vma=False,
    )
```

```python
import math

import numpy as np
import jax
import jax.numpy as jnp
from jax import lax
from jax.sharding import PartitionSpec as P

TPL = 256


WAVELENGTH = 0.0197
AMPLITUDE = 0.07
mode = lax.Precision.HIGH


def padded(shard, sides, width):
    for axis, dim in sides:
        size, length = (lax.axis_size(axis), shard.shape[dim])
        up = [(i, (i + 1) % size) for i in range(size - 1)]
        down = [(j, i) for i, j in up]
        last = lax.slice_in_dim(shard, length - width, length, axis=dim)
        initial = lax.slice_in_dim(shard, 0, width, axis=dim)
        before = lax.ppermute(last, axis, up)
        after = lax.ppermute(initial, axis, down)
        shard = jnp.concatenate([before, shard, after], axis=dim)
    return shard


def product(former, latter):
    return jnp.dot(former, latter, precision=mode, preferred_element_type=jnp.float32)


def tables(tile_width, margin, extent):
    n = tile_width + 2 * margin
    h = n // 2 + 1
    idx = np.arange(n)
    angles = 2.0 * np.pi * ((idx[:, None] * idx[None, :]) % n) / n
    cos, sin = np.cos(angles), np.sin(angles)
    left = np.concatenate([cos[:h], sin[1:h - 1]], axis=0)
    left_t = left[:, :extent]
    window_cols = slice(margin, margin + tile_width)
    right_w = np.concatenate([cos[window_cols, :h], sin[window_cols, 1:h - 1]], axis=1)
    right_t = np.concatenate([cos[:extent, :h], sin[:extent, 1:h - 1]], axis=1)
    mirror = np.concatenate([np.arange(h), n - np.arange(1, h - 1)])
    back = np.concatenate([cos[mirror, :tile_width], sin[mirror, :tile_width]], axis=1)
    weight = np.full(h, 2.0)
    weight[0] = 1.0
    weight[-1] = 1.0
    final = np.concatenate(
        [cos[:tile_width, :h] * weight, -2.0 * sin[:tile_width, 1:h - 1]], axis=1
    ) / (n * n)
    as32 = lambda a: jnp.asarray(a.astype(np.float32))
    return tuple(as32(a) for a in (left, left_t, right_w, right_t, back, final))


def per_device(micrograph, templates, defocus_values, defocus_group):
    tile_rows, tile_width = micrograph.shape
    margin = TPL // 2
    n = tile_width + 2 * margin
    h = n // 2 + 1
    tile_count = lax.axis_size("tile")
    pixel_count = float(tile_rows * tile_width * tile_count)
    own_rows, tpl_width = templates.shape[1], templates.shape[2]
    halo = padded(micrograph, (("tile", 0),), margin)
    lane = lax.broadcasted_iota(jnp.int32, (1, tpl_width), 1)
    half = tpl_width // 2
    stats_row = jnp.where(lane < half, jnp.sum(micrograph), jnp.sum(micrograph * micrograph))
    payload = jnp.concatenate([templates[0], stats_row], axis=0)
    everything = lax.all_gather(payload, "tile")
    totals = jnp.sum(everything[:, own_rows, :], axis=0)
    gathered = everything[:, :own_rows].reshape(tile_count * own_rows, tpl_width)
    centre = totals[:half] / pixel_count
    spread = jnp.sqrt(totals[half:] / pixel_count - centre * centre + 1e-05)
    reps = tile_width // half
    centre, spread = jnp.tile(centre, reps)[None, :], jnp.tile(spread, reps)[None, :]
    tile_index = lax.axis_index("tile")
    row_ids = lax.broadcasted_iota(jnp.int32, (n, 1), 0)
    valid = ((row_ids >= margin) | (tile_index > 0)) & (
        (row_ids < margin + tile_rows) | (tile_index < tile_count - 1)
    )
    rows_ext = lax.optimization_barrier(jnp.where(valid, (halo - centre) / spread, 0.0))
    extent = gathered.shape[0]
    left, left_t, right_w, right_t, back, final = tables(tile_width, margin, extent)

    centred = gathered - jnp.mean(gathered)
    root_mean = jnp.sqrt(jnp.mean(centred * centred) + 1e-06)
    normed = centred / (root_mean * TPL)

    edge_rows, edge_cols = ((1, 1), (0, 0)), ((0, 0), (1, 1))

    def halves(packed):
        return packed[:h], jnp.pad(packed[h:], edge_rows)

    def direct(ga, gb):
        ga_s, gb_s = jnp.pad(ga[:, h:], edge_cols), jnp.pad(gb[:, h:], edge_cols)
        return ga[:, :h] - gb_s, -(ga_s + gb[:, :h])

    def mirrored(ga, gb):
        return ga[:, 1:h - 1] + gb[:, h:], ga[:, h:] - gb[:, 1:h - 1]

    window_parts = halves(product(product(left, rows_ext), right_w))
    template_parts = halves(product(product(left_t, normed), right_t))

    positions = lax.iota(jnp.int32, n)
    signed_freq = (
        jnp.where(positions < n // 2, positions, positions - n).astype(jnp.float32) / n
    )
    packed_freq = jnp.where(positions < h, positions, positions - (h - 1)).astype(jnp.float32) / n
    group_ids = lax.iota(jnp.int32, defocus_values.shape[0])
    defocus = jnp.sum(jnp.where(group_ids == defocus_group[0], defocus_values, 0.0))
    scale = math.pi * WAVELENGTH * defocus
    row_phase = scale * signed_freq[:h, None] ** 2
    col_phase = scale * packed_freq[None, :] ** 2
    sin_r, cos_r = jnp.sin(row_phase), jnp.cos(row_phase)
    sin_c, cos_c = jnp.sin(col_phase), jnp.cos(col_phase)
    weight_sin = math.sqrt(1.0 - AMPLITUDE * AMPLITUDE)
    col_u = weight_sin * cos_c - AMPLITUDE * sin_c
    col_v = weight_sin * sin_c + AMPLITUDE * cos_c
    contrast = -(sin_r * col_u + cos_r * col_v)
    def multiply(form, weight):
        spec_real, spec_imag = form(*window_parts)
        template_real, template_imag = form(*template_parts)
        return (
            (spec_real * template_real + spec_imag * template_imag) * weight,
            (spec_imag * template_real - spec_real * template_imag) * weight,
        )

    real_d, imag_d = multiply(direct, contrast[:, :h])
    real_m, imag_m = multiply(mirrored, contrast[:, h:])
    lhs = jnp.concatenate(
        [jnp.concatenate([real_d, real_m], axis=1), jnp.concatenate([imag_d, imag_m], axis=1)],
        axis=0,
    )
    inner = product(lhs, back)
    pr_c, pr_s = inner[:h, :tile_width], inner[:h, tile_width:]
    pi_c, pi_s = inner[h:, :tile_width], inner[h:, tile_width:]
    back_real = pr_c - pi_s
    back_imag = pr_s + pi_c
    scores = product(final, jnp.concatenate([back_real, back_imag[1:h - 1]], axis=0))

    orient_count = lax.axis_size("orient")
    share_rows = tile_rows // orient_count
    pieces = lax.all_to_all(scores, "orient", 0, 0, tiled=True).reshape(
        orient_count, share_rows, tile_width
    )
    top = pieces[0]
    second = jnp.full_like(top, -jnp.inf)
    total = pieces[0]
    squares = pieces[0] * pieces[0]
    for k in range(1, orient_count):
        value = pieces[k]
        second = jnp.maximum(second, jnp.minimum(top, value))
        top = jnp.maximum(top, value)
        total = total + value
        squares = squares + value * value
    mean_map = total / orient_count
    variance = squares / orient_count - mean_map * mean_map
    return (top, second, mean_map, variance)


def solution(mesh):
    placed = (P("tile", None), P("orient", "tile", None), P(), P("tile"))
    return jax.shard_map(
        per_device,
        mesh=mesh,
        in_specs=placed,
        out_specs=(
            P(("tile", "orient"), None),
            P(("tile", "orient"), None),
            P(("tile", "orient"), None),
            P(("tile", "orient"), None),
        ),
        check_vma=False,
    )
```

```python
import math

import numpy as np
import jax
import jax.numpy as jnp
from jax import lax
from jax.sharding import PartitionSpec as P

TPL = 256


WAVELENGTH = 0.0197
AMPLITUDE = 0.07
mode = lax.Precision.HIGH


def padded(shard, sides, width):
    for axis, dim in sides:
        size, length = (lax.axis_size(axis), shard.shape[dim])
        up = [(i, (i + 1) % size) for i in range(size - 1)]
        down = [(j, i) for i, j in up]
        last = lax.slice_in_dim(shard, length - width, length, axis=dim)
        initial = lax.slice_in_dim(shard, 0, width, axis=dim)
        before = lax.ppermute(last, axis, up)
        after = lax.ppermute(initial, axis, down)
        shard = jnp.concatenate([before, shard, after], axis=dim)
    return shard


def product(former, latter):
    return jnp.dot(former, latter, precision=mode, preferred_element_type=jnp.float32)


def tables(tile_width, margin, extent):
    n = tile_width + 2 * margin
    h = n // 2 + 1
    idx = np.arange(n)
    angles = 2.0 * np.pi * ((idx[:, None] * idx[None, :]) % n) / n
    cos, sin = np.cos(angles), np.sin(angles)
    left = np.concatenate([cos[:h], sin[1:h - 1]], axis=0)
    left_t = left[:, :extent]
    window_cols = slice(margin, margin + tile_width)
    right_w = np.concatenate([cos[window_cols, :h], sin[window_cols, 1:h - 1]], axis=1)
    right_t = np.concatenate([cos[:extent, :h], sin[:extent, 1:h - 1]], axis=1)
    mirror = np.concatenate([np.arange(h), n - np.arange(1, h - 1)])
    back = np.concatenate([cos[mirror, :tile_width], sin[mirror, :tile_width]], axis=1)
    weight = np.full(h, 2.0)
    weight[0] = 1.0
    weight[-1] = 1.0
    final = np.concatenate(
        [cos[:tile_width, :h] * weight, -2.0 * sin[:tile_width, 1:h - 1]], axis=1
    ) / (n * n)
    as32 = lambda a: jnp.asarray(a.astype(np.float32))
    return tuple(as32(a) for a in (left, left_t, right_w, right_t, back, final))


def per_device(micrograph, templates, defocus_values, defocus_group):
    tile_rows, tile_width = micrograph.shape
    margin = TPL // 2
    n = tile_width + 2 * margin
    h = n // 2 + 1
    tile_count = lax.axis_size("tile")
    pixel_count = float(tile_rows * tile_width * tile_count)
    own_rows, tpl_width = templates.shape[1], templates.shape[2]
    halo = padded(micrograph, (("tile", 0),), margin)
    lane = lax.broadcasted_iota(jnp.int32, (1, tpl_width), 1)
    half = tpl_width // 2
    stats_row = jnp.where(lane < half, jnp.sum(micrograph), jnp.sum(micrograph * micrograph))
    payload = jnp.concatenate([templates[0], stats_row], axis=0)
    everything = lax.all_gather(payload, "tile")
    totals = jnp.sum(everything[:, own_rows, :], axis=0)
    gathered = everything[:, :own_rows].reshape(tile_count * own_rows, tpl_width)
    centre = totals[:half] / pixel_count
    spread = jnp.sqrt(totals[half:] / pixel_count - centre * centre + 1e-05)
    reps = tile_width // half
    centre, spread = jnp.tile(centre, reps)[None, :], jnp.tile(spread, reps)[None, :]
    tile_index = lax.axis_index("tile")
    row_ids = lax.broadcasted_iota(jnp.int32, (n, 1), 0)
    valid = ((row_ids >= margin) | (tile_index > 0)) & (
        (row_ids < margin + tile_rows) | (tile_index < tile_count - 1)
    )
    rows_ext = lax.optimization_barrier(jnp.where(valid, (halo - centre) / spread, 0.0))
    extent = gathered.shape[0]
    left, left_t, right_w, right_t, back, final = tables(tile_width, margin, extent)

    def lane_total(columns):
        width = columns.shape[0]
        if width & (width - 1):
            return jnp.full((1, width), jnp.sum(columns))
        step = width // 2
        while step:
            columns = columns + jnp.roll(columns, step)
            step //= 2
        return columns[None, :]

    tpl_count = float(gathered.shape[0] * gathered.shape[1])
    centred = gathered - lane_total(jnp.sum(gathered, axis=0)) / tpl_count
    root_mean = jnp.sqrt(lane_total(jnp.sum(centred * centred, axis=0)) / tpl_count + 1e-06)
    normed = centred / (root_mean * TPL)

    edge_rows, edge_cols = ((1, 1), (0, 0)), ((0, 0), (1, 1))

    def halves(packed):
        return packed[:h], jnp.pad(packed[h:], edge_rows)

    def direct(ga, gb):
        ga_s, gb_s = jnp.pad(ga[:, h:], edge_cols), jnp.pad(gb[:, h:], edge_cols)
        return ga[:, :h] - gb_s, -(ga_s + gb[:, :h])

    def mirrored(ga, gb):
        return ga[:, 1:h - 1] + gb[:, h:], ga[:, h:] - gb[:, 1:h - 1]

    window_parts = halves(product(product(left, rows_ext), right_w))
    template_parts = halves(product(product(left_t, normed), right_t))

    positions = lax.iota(jnp.int32, n)
    signed_freq = (
        jnp.where(positions < n // 2, positions, positions - n).astype(jnp.float32) / n
    )
    packed_freq = jnp.where(positions < h, positions, positions - (h - 1)).astype(jnp.float32) / n
    group_ids = lax.iota(jnp.int32, defocus_values.shape[0])
    defocus = jnp.sum(jnp.where(group_ids == defocus_group[0], defocus_values, 0.0))
    scale = math.pi * WAVELENGTH * defocus
    row_phase = scale * signed_freq[:h, None] ** 2
    col_phase = scale * packed_freq[None, :] ** 2
    sin_r, cos_r = jnp.sin(row_phase), jnp.cos(row_phase)
    sin_c, cos_c = jnp.sin(col_phase), jnp.cos(col_phase)
    weight_sin = math.sqrt(1.0 - AMPLITUDE * AMPLITUDE)
    col_u = weight_sin * cos_c - AMPLITUDE * sin_c
    col_v = weight_sin * sin_c + AMPLITUDE * cos_c
    contrast = -(sin_r * col_u + cos_r * col_v)
    def multiply(form, weight):
        spec_real, spec_imag = form(*window_parts)
        template_real, template_imag = form(*template_parts)
        return (
            (spec_real * template_real + spec_imag * template_imag) * weight,
            (spec_imag * template_real - spec_real * template_imag) * weight,
        )

    real_d, imag_d = multiply(direct, contrast[:, :h])
    real_m, imag_m = multiply(mirrored, contrast[:, h:])
    lhs = jnp.concatenate(
        [jnp.concatenate([real_d, real_m], axis=1), jnp.concatenate([imag_d, imag_m], axis=1)],
        axis=0,
    )
    inner = product(lhs, back)
    pr_c, pr_s = inner[:h, :tile_width], inner[:h, tile_width:]
    pi_c, pi_s = inner[h:, :tile_width], inner[h:, tile_width:]
    back_real = pr_c - pi_s
    back_imag = pr_s + pi_c
    scores = product(final, jnp.concatenate([back_real, back_imag[1:h - 1]], axis=0))

    orient_count = lax.axis_size("orient")
    share_rows = tile_rows // orient_count
    pieces = lax.all_to_all(scores, "orient", 0, 0, tiled=True).reshape(
        orient_count, share_rows, tile_width
    )
    top = pieces[0]
    second = jnp.full_like(top, -jnp.inf)
    total = pieces[0]
    squares = pieces[0] * pieces[0]
    for k in range(1, orient_count):
        value = pieces[k]
        second = jnp.maximum(second, jnp.minimum(top, value))
        top = jnp.maximum(top, value)
        total = total + value
        squares = squares + value * value
    mean_map = total / orient_count
    variance = squares / orient_count - mean_map * mean_map
    return (top, second, mean_map, variance)


def solution(mesh):
    placed = (P("tile", None), P("orient", "tile", None), P(), P("tile"))
    return jax.shard_map(
        per_device,
        mesh=mesh,
        in_specs=placed,
        out_specs=(
            P(("tile", "orient"), None),
            P(("tile", "orient"), None),
            P(("tile", "orient"), None),
            P(("tile", "orient"), None),
        ),
        check_vma=False,
    )
```

```python
import math

import numpy as np
import jax
import jax.numpy as jnp
from jax import lax
from jax.sharding import PartitionSpec as P

TPL = 256


WAVELENGTH = 0.0197
AMPLITUDE = 0.07
mode = lax.Precision.HIGH


def padded(shard, sides, width):
    for axis, dim in sides:
        size, length = (lax.axis_size(axis), shard.shape[dim])
        up = [(i, (i + 1) % size) for i in range(size - 1)]
        down = [(j, i) for i, j in up]
        last = lax.slice_in_dim(shard, length - width, length, axis=dim)
        initial = lax.slice_in_dim(shard, 0, width, axis=dim)
        before = lax.ppermute(last, axis, up)
        after = lax.ppermute(initial, axis, down)
        shard = jnp.concatenate([before, shard, after], axis=dim)
    return shard


def product(former, latter):
    return jnp.dot(former, latter, precision=mode, preferred_element_type=jnp.float32)


def tables(tile_width, margin, extent):
    n = tile_width + 2 * margin
    h = n // 2 + 1
    idx = np.arange(n)
    angles = 2.0 * np.pi * ((idx[:, None] * idx[None, :]) % n) / n
    cos, sin = np.cos(angles), np.sin(angles)
    left = np.concatenate([cos[:h], sin[1:h - 1]], axis=0)
    left_t = left[:, :extent]
    window_cols = slice(margin, margin + tile_width)
    right_w = np.concatenate([cos[window_cols, :h], sin[window_cols, 1:h - 1]], axis=1)
    right_t = np.concatenate([cos[:extent, :h], sin[:extent, 1:h - 1]], axis=1)
    mirror = np.concatenate([np.arange(h), n - np.arange(1, h - 1)])
    back = np.concatenate([cos[mirror, :tile_width], sin[mirror, :tile_width]], axis=1)
    weight = np.full(h, 2.0)
    weight[0] = 1.0
    weight[-1] = 1.0
    final = np.concatenate(
        [cos[:tile_width, :h] * weight, -2.0 * sin[:tile_width, 1:h - 1]], axis=1
    ) / (n * n)
    as32 = lambda a: jnp.asarray(a.astype(np.float32))
    return tuple(as32(a) for a in (left, left_t, right_w, right_t, back, final))


def per_device(micrograph, templates, defocus_values, defocus_group):
    tile_rows, tile_width = micrograph.shape
    margin = TPL // 2
    n = tile_width + 2 * margin
    h = n // 2 + 1
    tile_count = lax.axis_size("tile")
    pixel_count = float(tile_rows * tile_width * tile_count)
    own_rows, tpl_width = templates.shape[1], templates.shape[2]
    halo = padded(micrograph, (("tile", 0),), margin)
    lane = lax.broadcasted_iota(jnp.int32, (1, tpl_width), 1)
    half = tpl_width // 2
    stats_row = jnp.where(lane < half, jnp.sum(micrograph), jnp.sum(micrograph * micrograph))
    payload = jnp.concatenate([templates[0], stats_row], axis=0)
    everything = lax.all_gather(payload, "tile")
    totals = jnp.sum(everything[:, own_rows, :], axis=0)
    gathered = everything[:, :own_rows].reshape(tile_count * own_rows, tpl_width)
    centre = totals[:half] / pixel_count
    spread = jnp.sqrt(totals[half:] / pixel_count - centre * centre + 1e-05)
    reps = tile_width // half
    centre, spread = jnp.tile(centre, reps)[None, :], jnp.tile(spread, reps)[None, :]
    tile_index = lax.axis_index("tile")
    row_ids = lax.broadcasted_iota(jnp.int32, (n, 1), 0)
    valid = ((row_ids >= margin) | (tile_index > 0)) & (
        (row_ids < margin + tile_rows) | (tile_index < tile_count - 1)
    )
    rows_ext = lax.optimization_barrier(jnp.where(valid, (halo - centre) / spread, 0.0))
    extent = gathered.shape[0]
    left, left_t, right_w, right_t, back, final = tables(tile_width, margin, extent)

    centred = gathered - jnp.mean(gathered)
    root_mean = jnp.sqrt(jnp.mean(centred * centred) + 1e-06)
    normed = centred / (root_mean * TPL)

    edge_rows, edge_cols = ((1, 1), (0, 0)), ((0, 0), (1, 1))

    def halves(packed):
        return packed[:h], jnp.pad(packed[h:], edge_rows)

    def direct(ga, gb):
        ga_s, gb_s = jnp.pad(ga[:, h:], edge_cols), jnp.pad(gb[:, h:], edge_cols)
        return ga[:, :h] - gb_s, -(ga_s + gb[:, :h])

    def mirrored(ga, gb):
        return ga[:, 1:h - 1] + gb[:, h:], ga[:, h:] - gb[:, 1:h - 1]

    window_parts = halves(product(product(left, rows_ext), right_w))
    template_parts = halves(product(product(left_t, normed), right_t))

    positions = lax.iota(jnp.int32, n)
    signed_freq = (
        jnp.where(positions < n // 2, positions, positions - n).astype(jnp.float32) / n
    )
    packed_freq = jnp.where(positions < h, positions, positions - (h - 1)).astype(jnp.float32) / n
    group_ids = lax.iota(jnp.int32, defocus_values.shape[0])
    defocus = jnp.sum(jnp.where(group_ids == defocus_group[0], defocus_values, 0.0))
    scale = math.pi * WAVELENGTH * defocus
    row_phase = scale * signed_freq[:h, None] ** 2
    col_phase = scale * packed_freq[None, :] ** 2
    sin_r, cos_r = jnp.sin(row_phase), jnp.cos(row_phase)
    sin_c, cos_c = jnp.sin(col_phase), jnp.cos(col_phase)
    weight_sin = math.sqrt(1.0 - AMPLITUDE * AMPLITUDE)
    col_u = weight_sin * cos_c - AMPLITUDE * sin_c
    col_v = weight_sin * sin_c + AMPLITUDE * cos_c
    contrast = -(sin_r * col_u + cos_r * col_v)
    def multiply(form, weight):
        spec_real, spec_imag = form(*window_parts)
        template_real, template_imag = form(*template_parts)
        return (
            (spec_real * template_real + spec_imag * template_imag) * weight,
            (spec_imag * template_real - spec_real * template_imag) * weight,
        )

    real_d, imag_d = multiply(direct, contrast[:, :h])
    real_m, imag_m = multiply(mirrored, contrast[:, h:])
    lhs = jnp.concatenate(
        [jnp.concatenate([real_d, real_m], axis=1), jnp.concatenate([imag_d, imag_m], axis=1)],
        axis=0,
    )
    inner = product(lhs, back)
    pr_c, pr_s = inner[:h, :tile_width], inner[:h, tile_width:]
    pi_c, pi_s = inner[h:, :tile_width], inner[h:, tile_width:]
    back_real = pr_c - pi_s
    back_imag = pr_s + pi_c
    scores = product(final, jnp.concatenate([back_real, back_imag[1:h - 1]], axis=0))

    orient_count = lax.axis_size("orient")
    share_rows = tile_rows // orient_count
    pieces = lax.all_to_all(scores, "orient", 0, 0, tiled=True).reshape(
        orient_count, share_rows, tile_width
    )
    def merge(former, latter):
        return (
            jnp.maximum(former[0], latter[0]),
            jnp.maximum(jnp.minimum(former[0], latter[0]), jnp.maximum(former[1], latter[1])),
            former[2] + latter[2],
            former[3] + latter[3],
        )

    lowest = jnp.float32(-jnp.inf)
    top, second, total, squares = lax.reduce(
        (pieces, jnp.full_like(pieces, lowest), pieces, pieces * pieces),
        (lowest, lowest, jnp.float32(0.0), jnp.float32(0.0)),
        merge,
        (0,),
    )
    mean_map = total / orient_count
    variance = squares / orient_count - mean_map * mean_map
    return (top, second, mean_map, variance)


def solution(mesh):
    placed = (P("tile", None), P("orient", "tile", None), P(), P("tile"))
    return jax.shard_map(
        per_device,
        mesh=mesh,
        in_specs=placed,
        out_specs=(
            P(("tile", "orient"), None),
            P(("tile", "orient"), None),
            P(("tile", "orient"), None),
            P(("tile", "orient"), None),
        ),
        check_vma=False,
    )
```

```python
import math

import numpy as np
import jax
import jax.numpy as jnp
from jax import lax
from jax.sharding import PartitionSpec as P

TPL = 256


WAVELENGTH = 0.0197
AMPLITUDE = 0.07
mode = lax.Precision.HIGH


def padded(shard, sides, width):
    for axis, dim in sides:
        size, length = (lax.axis_size(axis), shard.shape[dim])
        up = [(i, (i + 1) % size) for i in range(size - 1)]
        down = [(j, i) for i, j in up]
        last = lax.slice_in_dim(shard, length - width, length, axis=dim)
        initial = lax.slice_in_dim(shard, 0, width, axis=dim)
        before = lax.ppermute(last, axis, up)
        after = lax.ppermute(initial, axis, down)
        shard = jnp.concatenate([before, shard, after], axis=dim)
    return shard


def product(former, latter):
    return jnp.dot(former, latter, precision=mode, preferred_element_type=jnp.float32)


def tables(tile_width, margin, extent):
    n = tile_width + 2 * margin
    h = n // 2 + 1
    idx = np.arange(n)
    angles = 2.0 * np.pi * ((idx[:, None] * idx[None, :]) % n) / n
    cos, sin = np.cos(angles), np.sin(angles)
    left = np.concatenate([cos[:h], sin[1:h - 1]], axis=0)
    left_t = left[:, :extent]
    window_cols = slice(margin, margin + tile_width)
    right_w = np.concatenate([cos[window_cols, :h], sin[window_cols, 1:h - 1]], axis=1)
    right_t = np.concatenate([cos[:extent, :h], sin[:extent, 1:h - 1]], axis=1)
    mirror = np.concatenate([np.arange(h), n - np.arange(1, h - 1)])
    back = np.concatenate([cos[mirror, :tile_width], sin[mirror, :tile_width]], axis=1)
    weight = np.full(h, 2.0)
    weight[0] = 1.0
    weight[-1] = 1.0
    final = np.concatenate(
        [cos[:tile_width, :h] * weight, -2.0 * sin[:tile_width, 1:h - 1]], axis=1
    ) / (n * n)
    as32 = lambda a: jnp.asarray(a.astype(np.float32))
    return tuple(as32(a) for a in (left, left_t, right_w, right_t, back, final))


def per_device(micrograph, templates, defocus_values, defocus_group):
    tile_rows, tile_width = micrograph.shape
    margin = TPL // 2
    n = tile_width + 2 * margin
    h = n // 2 + 1
    tile_count = lax.axis_size("tile")
    pixel_count = float(tile_rows * tile_width * tile_count)
    own_rows, tpl_width = templates.shape[1], templates.shape[2]
    halo = padded(micrograph, (("tile", 0),), margin)
    lane = lax.broadcasted_iota(jnp.int32, (1, tpl_width), 1)
    half = tpl_width // 2
    stats_row = jnp.where(lane < half, jnp.sum(micrograph), jnp.sum(micrograph * micrograph))
    payload = jnp.concatenate([templates[0], stats_row], axis=0)
    everything = lax.all_gather(payload, "tile")
    totals = jnp.sum(everything[:, own_rows, :], axis=0)
    gathered = everything[:, :own_rows].reshape(tile_count * own_rows, tpl_width)
    centre = totals[:half] / pixel_count
    spread = jnp.sqrt(totals[half:] / pixel_count - centre * centre + 1e-05)
    reps = tile_width // half
    centre, spread = jnp.tile(centre, reps)[None, :], jnp.tile(spread, reps)[None, :]
    tile_index = lax.axis_index("tile")
    row_ids = lax.broadcasted_iota(jnp.int32, (n, 1), 0)
    valid = ((row_ids >= margin) | (tile_index > 0)) & (
        (row_ids < margin + tile_rows) | (tile_index < tile_count - 1)
    )
    rows_ext = lax.optimization_barrier(jnp.where(valid, (halo - centre) / spread, 0.0))
    extent = gathered.shape[0]
    left, left_t, right_w, right_t, back, final = tables(tile_width, margin, extent)

    tpl_count = float(gathered.shape[0] * gathered.shape[1])
    ones = jnp.ones((gathered.shape[1], gathered.shape[1]), jnp.float32)

    def lane_total(rows):
        return jnp.dot(
            jnp.sum(rows, axis=0, keepdims=True), ones,
            precision=lax.Precision.HIGHEST, preferred_element_type=jnp.float32,
        )

    centred = gathered - lane_total(gathered) / tpl_count
    root_mean = jnp.sqrt(lane_total(centred * centred) / tpl_count + 1e-06)
    normed = centred / (root_mean * TPL)

    edge_rows, edge_cols = ((1, 1), (0, 0)), ((0, 0), (1, 1))

    def halves(packed):
        return packed[:h], jnp.pad(packed[h:], edge_rows)

    def direct(ga, gb):
        ga_s, gb_s = jnp.pad(ga[:, h:], edge_cols), jnp.pad(gb[:, h:], edge_cols)
        return ga[:, :h] - gb_s, -(ga_s + gb[:, :h])

    def mirrored(ga, gb):
        return ga[:, 1:h - 1] + gb[:, h:], ga[:, h:] - gb[:, 1:h - 1]

    window_parts = halves(product(product(left, rows_ext), right_w))
    template_parts = halves(product(product(left_t, normed), right_t))

    positions = lax.iota(jnp.int32, n)
    signed_freq = (
        jnp.where(positions < n // 2, positions, positions - n).astype(jnp.float32) / n
    )
    packed_freq = jnp.where(positions < h, positions, positions - (h - 1)).astype(jnp.float32) / n
    group_ids = lax.iota(jnp.int32, defocus_values.shape[0])
    defocus = jnp.sum(jnp.where(group_ids == defocus_group[0], defocus_values, 0.0))
    scale = math.pi * WAVELENGTH * defocus
    row_phase = scale * signed_freq[:h, None] ** 2
    col_phase = scale * packed_freq[None, :] ** 2
    sin_r, cos_r = jnp.sin(row_phase), jnp.cos(row_phase)
    sin_c, cos_c = jnp.sin(col_phase), jnp.cos(col_phase)
    weight_sin = math.sqrt(1.0 - AMPLITUDE * AMPLITUDE)
    col_u = weight_sin * cos_c - AMPLITUDE * sin_c
    col_v = weight_sin * sin_c + AMPLITUDE * cos_c
    contrast = -(sin_r * col_u + cos_r * col_v)
    def multiply(form, weight):
        spec_real, spec_imag = form(*window_parts)
        template_real, template_imag = form(*template_parts)
        return (
            (spec_real * template_real + spec_imag * template_imag) * weight,
            (spec_imag * template_real - spec_real * template_imag) * weight,
        )

    real_d, imag_d = multiply(direct, contrast[:, :h])
    real_m, imag_m = multiply(mirrored, contrast[:, h:])
    lhs = jnp.concatenate(
        [jnp.concatenate([real_d, real_m], axis=1), jnp.concatenate([imag_d, imag_m], axis=1)],
        axis=0,
    )
    inner = product(lhs, back)
    pr_c, pr_s = inner[:h, :tile_width], inner[:h, tile_width:]
    pi_c, pi_s = inner[h:, :tile_width], inner[h:, tile_width:]
    back_real = pr_c - pi_s
    back_imag = pr_s + pi_c
    scores = product(final, jnp.concatenate([back_real, back_imag[1:h - 1]], axis=0))

    orient_count = lax.axis_size("orient")
    share_rows = tile_rows // orient_count
    pieces = lax.all_to_all(scores, "orient", 0, 0, tiled=True).reshape(
        orient_count, share_rows, tile_width
    )
    def merge(former, latter):
        return (
            jnp.maximum(former[0], latter[0]),
            jnp.maximum(jnp.minimum(former[0], latter[0]), jnp.maximum(former[1], latter[1])),
            former[2] + latter[2],
            former[3] + latter[3],
        )

    lowest = jnp.float32(-jnp.inf)
    top, second, total, squares = lax.reduce(
        (pieces, jnp.full_like(pieces, lowest), pieces, pieces * pieces),
        (lowest, lowest, jnp.float32(0.0), jnp.float32(0.0)),
        merge,
        (0,),
    )
    mean_map = total / orient_count
    variance = squares / orient_count - mean_map * mean_map
    return (top, second, mean_map, variance)


def solution(mesh):
    placed = (P("tile", None), P("orient", "tile", None), P(), P("tile"))
    return jax.shard_map(
        per_device,
        mesh=mesh,
        in_specs=placed,
        out_specs=(
            P(("tile", "orient"), None),
            P(("tile", "orient"), None),
            P(("tile", "orient"), None),
            P(("tile", "orient"), None),
        ),
        check_vma=False,
    )
```

```python
import math

import numpy as np
import jax
import jax.numpy as jnp
from jax import lax
from jax.sharding import PartitionSpec as P

TPL = 256


WAVELENGTH = 0.0197
AMPLITUDE = 0.07
mode = lax.Precision.HIGH


def padded(shard, sides, width):
    for axis, dim in sides:
        size, length = (lax.axis_size(axis), shard.shape[dim])
        up = [(i, (i + 1) % size) for i in range(size - 1)]
        down = [(j, i) for i, j in up]
        last = lax.slice_in_dim(shard, length - width, length, axis=dim)
        initial = lax.slice_in_dim(shard, 0, width, axis=dim)
        before = lax.ppermute(last, axis, up)
        after = lax.ppermute(initial, axis, down)
        shard = jnp.concatenate([before, shard, after], axis=dim)
    return shard


def product(former, latter):
    return jnp.dot(former, latter, precision=mode, preferred_element_type=jnp.float32)


def tables(tile_width, margin, extent):
    n = tile_width + 2 * margin
    h = n // 2 + 1
    idx = np.arange(n)
    angles = 2.0 * np.pi * ((idx[:, None] * idx[None, :]) % n) / n
    cos, sin = np.cos(angles), np.sin(angles)
    left = np.concatenate([cos[:h], sin[1:h - 1]], axis=0)
    left_t = left[:, :extent]
    window_cols = slice(margin, margin + tile_width)
    right_w = np.concatenate([cos[window_cols, :h], sin[window_cols, 1:h - 1]], axis=1)
    right_t = np.concatenate([cos[:extent, :h], sin[:extent, 1:h - 1]], axis=1)
    mirror = np.concatenate([np.arange(h), n - np.arange(1, h - 1)])
    back = np.concatenate([cos[mirror, :tile_width], sin[mirror, :tile_width]], axis=1)
    weight = np.full(h, 2.0)
    weight[0] = 1.0
    weight[-1] = 1.0
    final = np.concatenate(
        [cos[:tile_width, :h] * weight, -2.0 * sin[:tile_width, 1:h - 1]], axis=1
    ) / (n * n)
    as32 = lambda a: jnp.asarray(a.astype(np.float32))
    return tuple(as32(a) for a in (left, left_t, right_w, right_t, back, final))


def per_device(micrograph, templates, defocus_values, defocus_group):
    tile_rows, tile_width = micrograph.shape
    margin = TPL // 2
    n = tile_width + 2 * margin
    h = n // 2 + 1
    tile_count = lax.axis_size("tile")
    pixel_count = float(tile_rows * tile_width * tile_count)
    own_rows, tpl_width = templates.shape[1], templates.shape[2]
    halo = padded(micrograph, (("tile", 0),), margin)
    def lane_fold(columns):
        return sum(columns[i:i + tpl_width] for i in range(0, tile_width, tpl_width))[None, :]

    sum_row = lane_fold(jnp.sum(micrograph, axis=0))
    square_row = lane_fold(jnp.sum(micrograph * micrograph, axis=0))
    payload = jnp.concatenate([templates[0], sum_row, square_row], axis=0)
    everything = lax.all_gather(payload, "tile")
    gathered = everything[:, :own_rows].reshape(tile_count * own_rows, tpl_width)
    ones = jnp.ones((tpl_width, tpl_width), jnp.float32)

    def lane_total(rows):
        return jnp.dot(
            jnp.sum(rows, axis=0, keepdims=True), ones,
            precision=lax.Precision.HIGHEST, preferred_element_type=jnp.float32,
        )

    centre = lane_total(everything[:, own_rows]) / pixel_count
    spread = jnp.sqrt(lane_total(everything[:, own_rows + 1]) / pixel_count - centre * centre + 1e-05)
    reps = tile_width // tpl_width
    centre, spread = jnp.tile(centre, (1, reps)), jnp.tile(spread, (1, reps))
    tile_index = lax.axis_index("tile")
    row_ids = lax.broadcasted_iota(jnp.int32, (n, 1), 0)
    valid = ((row_ids >= margin) | (tile_index > 0)) & (
        (row_ids < margin + tile_rows) | (tile_index < tile_count - 1)
    )
    rows_ext = lax.optimization_barrier(jnp.where(valid, (halo - centre) / spread, 0.0))
    extent = gathered.shape[0]
    left, left_t, right_w, right_t, back, final = tables(tile_width, margin, extent)

    tpl_count = float(gathered.shape[0] * gathered.shape[1])
    centred = gathered - lane_total(gathered) / tpl_count
    root_mean = jnp.sqrt(lane_total(centred * centred) / tpl_count + 1e-06)
    normed = centred / (root_mean * TPL)

    edge_rows, edge_cols = ((1, 1), (0, 0)), ((0, 0), (1, 1))

    def halves(packed):
        return packed[:h], jnp.pad(packed[h:], edge_rows)

    def direct(ga, gb):
        ga_s, gb_s = jnp.pad(ga[:, h:], edge_cols), jnp.pad(gb[:, h:], edge_cols)
        return ga[:, :h] - gb_s, -(ga_s + gb[:, :h])

    def mirrored(ga, gb):
        return ga[:, 1:h - 1] + gb[:, h:], ga[:, h:] - gb[:, 1:h - 1]

    window_parts = halves(product(product(left, rows_ext), right_w))
    template_parts = halves(product(product(left_t, normed), right_t))

    positions = lax.iota(jnp.int32, n)
    signed_freq = (
        jnp.where(positions < n // 2, positions, positions - n).astype(jnp.float32) / n
    )
    packed_freq = jnp.where(positions < h, positions, positions - (h - 1)).astype(jnp.float32) / n
    group_ids = lax.iota(jnp.int32, defocus_values.shape[0])
    defocus = jnp.sum(jnp.where(group_ids == defocus_group[0], defocus_values, 0.0))
    scale = math.pi * WAVELENGTH * defocus
    row_phase = scale * signed_freq[:h, None] ** 2
    col_phase = scale * packed_freq[None, :] ** 2
    sin_r, cos_r = jnp.sin(row_phase), jnp.cos(row_phase)
    sin_c, cos_c = jnp.sin(col_phase), jnp.cos(col_phase)
    weight_sin = math.sqrt(1.0 - AMPLITUDE * AMPLITUDE)
    col_u = weight_sin * cos_c - AMPLITUDE * sin_c
    col_v = weight_sin * sin_c + AMPLITUDE * cos_c
    contrast = -(sin_r * col_u + cos_r * col_v)
    def multiply(form, weight):
        spec_real, spec_imag = form(*window_parts)
        template_real, template_imag = form(*template_parts)
        return (
            (spec_real * template_real + spec_imag * template_imag) * weight,
            (spec_imag * template_real - spec_real * template_imag) * weight,
        )

    real_d, imag_d = multiply(direct, contrast[:, :h])
    real_m, imag_m = multiply(mirrored, contrast[:, h:])
    lhs = jnp.concatenate(
        [jnp.concatenate([real_d, real_m], axis=1), jnp.concatenate([imag_d, imag_m], axis=1)],
        axis=0,
    )
    inner = product(lhs, back)
    pr_c, pr_s = inner[:h, :tile_width], inner[:h, tile_width:]
    pi_c, pi_s = inner[h:, :tile_width], inner[h:, tile_width:]
    back_real = pr_c - pi_s
    back_imag = pr_s + pi_c
    scores = product(final, jnp.concatenate([back_real, back_imag[1:h - 1]], axis=0))

    orient_count = lax.axis_size("orient")
    share_rows = tile_rows // orient_count
    pieces = lax.all_to_all(scores, "orient", 0, 0, tiled=True).reshape(
        orient_count, share_rows, tile_width
    )
    def merge(former, latter):
        return (
            jnp.maximum(former[0], latter[0]),
            jnp.maximum(jnp.minimum(former[0], latter[0]), jnp.maximum(former[1], latter[1])),
            former[2] + latter[2],
            former[3] + latter[3],
        )

    lowest = jnp.float32(-jnp.inf)
    top, second, total, squares = lax.reduce(
        (pieces, jnp.full_like(pieces, lowest), pieces, pieces * pieces),
        (lowest, lowest, jnp.float32(0.0), jnp.float32(0.0)),
        merge,
        (0,),
    )
    mean_map = total / orient_count
    variance = squares / orient_count - mean_map * mean_map
    return (top, second, mean_map, variance)


def solution(mesh):
    placed = (P("tile", None), P("orient", "tile", None), P(), P("tile"))
    return jax.shard_map(
        per_device,
        mesh=mesh,
        in_specs=placed,
        out_specs=(
            P(("tile", "orient"), None),
            P(("tile", "orient"), None),
            P(("tile", "orient"), None),
            P(("tile", "orient"), None),
        ),
        check_vma=False,
    )
```

```python
import math

import numpy as np
import jax
import jax.numpy as jnp
from jax import lax
from jax.sharding import PartitionSpec as P

TPL = 256


WAVELENGTH = 0.0197
AMPLITUDE = 0.07
mode = lax.Precision.HIGH


def padded(shard, sides, width):
    for axis, dim in sides:
        size, length = (lax.axis_size(axis), shard.shape[dim])
        up = [(i, (i + 1) % size) for i in range(size - 1)]
        down = [(j, i) for i, j in up]
        last = lax.slice_in_dim(shard, length - width, length, axis=dim)
        initial = lax.slice_in_dim(shard, 0, width, axis=dim)
        before = lax.ppermute(last, axis, up)
        after = lax.ppermute(initial, axis, down)
        shard = jnp.concatenate([before, shard, after], axis=dim)
    return shard


def product(former, latter):
    return jnp.dot(former, latter, precision=mode, preferred_element_type=jnp.float32)


def tables(tile_width, margin, extent):
    n = tile_width + 2 * margin
    h = n // 2 + 1
    idx = np.arange(n)
    angles = 2.0 * np.pi * ((idx[:, None] * idx[None, :]) % n) / n
    cos, sin = np.cos(angles), np.sin(angles)
    left = np.concatenate([cos[:h], sin[1:h - 1]], axis=0)
    left_t = left[:, :extent]
    window_cols = slice(margin, margin + tile_width)
    right_w = np.concatenate([cos[window_cols, :h], sin[window_cols, 1:h - 1]], axis=1)
    right_t = np.concatenate([cos[:extent, :h], sin[:extent, 1:h - 1]], axis=1)
    mirror = np.concatenate([np.arange(h), n - np.arange(1, h - 1)])
    back = np.concatenate([cos[mirror, :tile_width], sin[mirror, :tile_width]], axis=1)
    weight = np.full(h, 2.0)
    weight[0] = 1.0
    weight[-1] = 1.0
    final = np.concatenate(
        [cos[:tile_width, :h] * weight, -2.0 * sin[:tile_width, 1:h - 1]], axis=1
    ) / (n * n)
    as32 = lambda a: jnp.asarray(a.astype(np.float32))
    return tuple(as32(a) for a in (left, left_t, right_w, right_t, back, final))


def per_device(micrograph, templates, defocus_values, defocus_group):
    tile_rows, tile_width = micrograph.shape
    margin = TPL // 2
    n = tile_width + 2 * margin
    h = n // 2 + 1
    tile_count = lax.axis_size("tile")
    pixel_count = float(tile_rows * tile_width * tile_count)
    own_rows, tpl_width = templates.shape[1], templates.shape[2]
    def lane_fold(columns):
        return sum(columns[i:i + tpl_width] for i in range(0, tile_width, tpl_width))[None, :]

    sum_row = lane_fold(jnp.sum(micrograph, axis=0))
    square_row = lane_fold(jnp.sum(micrograph * micrograph, axis=0))
    payload = jnp.concatenate([templates[0], sum_row, square_row], axis=0)
    everything = lax.all_gather(payload, "tile")
    micrograph_after, everything = lax.optimization_barrier((micrograph, everything))
    halo = padded(micrograph_after, (("tile", 0),), margin)
    gathered = everything[:, :own_rows].reshape(tile_count * own_rows, tpl_width)
    ones = jnp.ones((tpl_width, tpl_width), jnp.float32)

    def lane_total(rows):
        return jnp.dot(
            jnp.sum(rows, axis=0, keepdims=True), ones,
            precision=lax.Precision.HIGHEST, preferred_element_type=jnp.float32,
        )

    centre = lane_total(everything[:, own_rows]) / pixel_count
    spread = jnp.sqrt(lane_total(everything[:, own_rows + 1]) / pixel_count - centre * centre + 1e-05)
    reps = tile_width // tpl_width
    centre, spread = jnp.tile(centre, (1, reps)), jnp.tile(spread, (1, reps))
    tile_index = lax.axis_index("tile")
    row_ids = lax.broadcasted_iota(jnp.int32, (n, 1), 0)
    valid = ((row_ids >= margin) | (tile_index > 0)) & (
        (row_ids < margin + tile_rows) | (tile_index < tile_count - 1)
    )
    rows_ext = lax.optimization_barrier(jnp.where(valid, (halo - centre) / spread, 0.0))
    extent = gathered.shape[0]
    left, left_t, right_w, right_t, back, final = tables(tile_width, margin, extent)

    tpl_count = float(gathered.shape[0] * gathered.shape[1])
    centred = gathered - lane_total(gathered) / tpl_count
    root_mean = jnp.sqrt(lane_total(centred * centred) / tpl_count + 1e-06)
    normed = centred / (root_mean * TPL)

    edge_rows, edge_cols = ((1, 1), (0, 0)), ((0, 0), (1, 1))

    def halves(packed):
        return packed[:h], jnp.pad(packed[h:], edge_rows)

    def direct(ga, gb):
        ga_s, gb_s = jnp.pad(ga[:, h:], edge_cols), jnp.pad(gb[:, h:], edge_cols)
        return ga[:, :h] - gb_s, -(ga_s + gb[:, :h])

    def mirrored(ga, gb):
        return ga[:, 1:h - 1] + gb[:, h:], ga[:, h:] - gb[:, 1:h - 1]

    window_parts = halves(product(product(left, rows_ext), right_w))
    template_parts = halves(product(product(left_t, normed), right_t))

    positions = lax.iota(jnp.int32, n)
    signed_freq = (
        jnp.where(positions < n // 2, positions, positions - n).astype(jnp.float32) / n
    )
    packed_freq = jnp.where(positions < h, positions, positions - (h - 1)).astype(jnp.float32) / n
    group_ids = lax.iota(jnp.int32, defocus_values.shape[0])
    defocus = jnp.sum(jnp.where(group_ids == defocus_group[0], defocus_values, 0.0))
    scale = math.pi * WAVELENGTH * defocus
    row_phase = scale * signed_freq[:h, None] ** 2
    col_phase = scale * packed_freq[None, :] ** 2
    sin_r, cos_r = jnp.sin(row_phase), jnp.cos(row_phase)
    sin_c, cos_c = jnp.sin(col_phase), jnp.cos(col_phase)
    weight_sin = math.sqrt(1.0 - AMPLITUDE * AMPLITUDE)
    col_u = weight_sin * cos_c - AMPLITUDE * sin_c
    col_v = weight_sin * sin_c + AMPLITUDE * cos_c
    contrast = -(sin_r * col_u + cos_r * col_v)
    def multiply(form, weight):
        spec_real, spec_imag = form(*window_parts)
        template_real, template_imag = form(*template_parts)
        return (
            (spec_real * template_real + spec_imag * template_imag) * weight,
            (spec_imag * template_real - spec_real * template_imag) * weight,
        )

    real_d, imag_d = multiply(direct, contrast[:, :h])
    real_m, imag_m = multiply(mirrored, contrast[:, h:])
    lhs = jnp.concatenate(
        [jnp.concatenate([real_d, real_m], axis=1), jnp.concatenate([imag_d, imag_m], axis=1)],
        axis=0,
    )
    inner = product(lhs, back)
    pr_c, pr_s = inner[:h, :tile_width], inner[:h, tile_width:]
    pi_c, pi_s = inner[h:, :tile_width], inner[h:, tile_width:]
    back_real = pr_c - pi_s
    back_imag = pr_s + pi_c
    scores = product(final, jnp.concatenate([back_real, back_imag[1:h - 1]], axis=0))

    orient_count = lax.axis_size("orient")
    share_rows = tile_rows // orient_count
    pieces = lax.all_to_all(scores, "orient", 0, 0, tiled=True).reshape(
        orient_count, share_rows, tile_width
    )
    def merge(former, latter):
        return (
            jnp.maximum(former[0], latter[0]),
            jnp.maximum(jnp.minimum(former[0], latter[0]), jnp.maximum(former[1], latter[1])),
            former[2] + latter[2],
            former[3] + latter[3],
        )

    lowest = jnp.float32(-jnp.inf)
    top, second, total, squares = lax.reduce(
        (pieces, jnp.full_like(pieces, lowest), pieces, pieces * pieces),
        (lowest, lowest, jnp.float32(0.0), jnp.float32(0.0)),
        merge,
        (0,),
    )
    mean_map = total / orient_count
    variance = squares / orient_count - mean_map * mean_map
    return (top, second, mean_map, variance)


def solution(mesh):
    placed = (P("tile", None), P("orient", "tile", None), P(), P("tile"))
    return jax.shard_map(
        per_device,
        mesh=mesh,
        in_specs=placed,
        out_specs=(
            P(("tile", "orient"), None),
            P(("tile", "orient"), None),
            P(("tile", "orient"), None),
            P(("tile", "orient"), None),
        ),
        check_vma=False,
    )
```

```python
import math

import numpy as np
import jax
import jax.numpy as jnp
from jax import lax
from jax.sharding import PartitionSpec as P

TPL = 256


WAVELENGTH = 0.0197
AMPLITUDE = 0.07
mode = lax.Precision.HIGH


def padded(shard, sides, width):
    for axis, dim in sides:
        size, length = (lax.axis_size(axis), shard.shape[dim])
        up = [(i, (i + 1) % size) for i in range(size - 1)]
        down = [(j, i) for i, j in up]
        last = lax.slice_in_dim(shard, length - width, length, axis=dim)
        initial = lax.slice_in_dim(shard, 0, width, axis=dim)
        before = lax.ppermute(last, axis, up)
        after = lax.ppermute(initial, axis, down)
        shard = jnp.concatenate([before, shard, after], axis=dim)
    return shard


def product(former, latter):
    return jnp.dot(former, latter, precision=mode, preferred_element_type=jnp.float32)


def tables(tile_width, margin, extent):
    n = tile_width + 2 * margin
    h = n // 2 + 1
    idx = np.arange(n)
    angles = 2.0 * np.pi * ((idx[:, None] * idx[None, :]) % n) / n
    cos, sin = np.cos(angles), np.sin(angles)
    left = np.concatenate([cos[:h], sin[1:h - 1]], axis=0)
    left_t = left[:, :extent]
    window_cols = slice(margin, margin + tile_width)
    right_w = np.concatenate([cos[window_cols, :h], sin[window_cols, 1:h - 1]], axis=1)
    right_t = np.concatenate([cos[:extent, :h], sin[:extent, 1:h - 1]], axis=1)
    mirror = np.concatenate([np.arange(h), n - np.arange(1, h - 1)])
    back = np.concatenate([cos[mirror, :tile_width], sin[mirror, :tile_width]], axis=1)
    weight = np.full(h, 2.0)
    weight[0] = 1.0
    weight[-1] = 1.0
    final = np.concatenate(
        [cos[:tile_width, :h] * weight, -2.0 * sin[:tile_width, 1:h - 1]], axis=1
    ) / (n * n)
    as32 = lambda a: jnp.asarray(a.astype(np.float32))
    return tuple(as32(a) for a in (left, left_t, right_w, right_t, back, final))


def per_device(micrograph, templates, defocus_values, defocus_group):
    tile_rows, tile_width = micrograph.shape
    margin = TPL // 2
    n = tile_width + 2 * margin
    h = n // 2 + 1
    tile_count = lax.axis_size("tile")
    pixel_count = float(tile_rows * tile_width * tile_count)
    own_rows, tpl_width = templates.shape[1], templates.shape[2]
    halo = padded(micrograph, (("tile", 0),), margin)
    def lane_fold(columns):
        return sum(columns[i:i + tpl_width] for i in range(0, tile_width, tpl_width))[None, :]

    sum_row = lane_fold(jnp.sum(micrograph, axis=0))
    square_row = lane_fold(jnp.sum(micrograph * micrograph, axis=0))
    payload = jnp.concatenate([templates[0], sum_row, square_row], axis=0)
    everything = lax.all_gather(payload, "tile")
    gathered = everything[:, :own_rows].reshape(tile_count * own_rows, tpl_width)
    ones = jnp.ones((tpl_width, tpl_width), jnp.float32)

    def lane_total(rows):
        return jnp.dot(
            jnp.sum(rows, axis=0, keepdims=True), ones,
            precision=lax.Precision.HIGHEST, preferred_element_type=jnp.float32,
        )

    centre = lane_total(everything[:, own_rows]) / pixel_count
    spread = jnp.sqrt(lane_total(everything[:, own_rows + 1]) / pixel_count - centre * centre + 1e-05)
    reps = tile_width // tpl_width
    centre, spread = jnp.tile(centre, (1, reps)), jnp.tile(spread, (1, reps))
    tile_index = lax.axis_index("tile")
    row_ids = lax.broadcasted_iota(jnp.int32, (n, 1), 0)
    valid = ((row_ids >= margin) | (tile_index > 0)) & (
        (row_ids < margin + tile_rows) | (tile_index < tile_count - 1)
    )
    rows_ext = lax.optimization_barrier(jnp.where(valid, (halo - centre) / spread, 0.0))
    extent = gathered.shape[0]
    left, left_t, right_w, right_t, back, final = tables(tile_width, margin, extent)

    tpl_count = float(gathered.shape[0] * gathered.shape[1])
    centred = gathered - lane_total(gathered) / tpl_count
    root_mean = jnp.sqrt(lane_total(centred * centred) / tpl_count + 1e-06)
    normed = centred / (root_mean * TPL)

    edge_rows, edge_cols = ((1, 1), (0, 0)), ((0, 0), (1, 1))

    def halves(packed):
        return packed[:h], jnp.pad(packed[h:], edge_rows)

    def direct(ga, gb):
        ga_s, gb_s = jnp.pad(ga[:, h:], edge_cols), jnp.pad(gb[:, h:], edge_cols)
        return ga[:, :h] - gb_s, -(ga_s + gb[:, :h])

    def mirrored(ga, gb):
        return ga[:, 1:h - 1] + gb[:, h:], ga[:, h:] - gb[:, 1:h - 1]

    window_parts = halves(product(product(left, rows_ext), right_w))
    template_parts = halves(product(product(left_t, normed), right_t))

    positions = lax.iota(jnp.int32, n)
    signed_freq = (
        jnp.where(positions < n // 2, positions, positions - n).astype(jnp.float32) / n
    )
    packed_freq = jnp.where(positions < h, positions, positions - (h - 1)).astype(jnp.float32) / n
    group_ids = lax.iota(jnp.int32, defocus_values.shape[0])
    defocus = jnp.sum(jnp.where(group_ids == defocus_group[0], defocus_values, 0.0))
    scale = math.pi * WAVELENGTH * defocus
    row_phase = scale * signed_freq[:h, None] ** 2
    col_phase = scale * packed_freq[None, :] ** 2
    sin_r, cos_r = jnp.sin(row_phase), jnp.cos(row_phase)
    sin_c, cos_c = jnp.sin(col_phase), jnp.cos(col_phase)
    weight_sin = math.sqrt(1.0 - AMPLITUDE * AMPLITUDE)
    col_u = weight_sin * cos_c - AMPLITUDE * sin_c
    col_v = weight_sin * sin_c + AMPLITUDE * cos_c
    contrast = -(sin_r * col_u + cos_r * col_v)
    def multiply(form, weight):
        spec_real, spec_imag = form(*window_parts)
        template_real, template_imag = form(*template_parts)
        return (
            (spec_real * template_real + spec_imag * template_imag) * weight,
            (spec_imag * template_real - spec_real * template_imag) * weight,
        )

    real_d, imag_d = multiply(direct, contrast[:, :h])
    real_m, imag_m = multiply(mirrored, contrast[:, h:])
    lhs = jnp.concatenate(
        [jnp.concatenate([real_d, real_m], axis=1), jnp.concatenate([imag_d, imag_m], axis=1)],
        axis=0,
    )
    orient_count = lax.axis_size("orient")
    share_rows = tile_rows // orient_count
    half_cols = tile_width // 2
    received = []
    for part in range(2):
        cols = slice(part * half_cols, (part + 1) * half_cols)
        back_part = jnp.concatenate(
            [back[:, cols], back[:, tile_width + part * half_cols:tile_width + (part + 1) * half_cols]],
            axis=1,
        )
        inner = product(lhs, back_part)
        pr_c, pr_s = inner[:h, :half_cols], inner[:h, half_cols:]
        pi_c, pi_s = inner[h:, :half_cols], inner[h:, half_cols:]
        back_real = pr_c - pi_s
        back_imag = pr_s + pi_c
        scores = product(final, jnp.concatenate([back_real, back_imag[1:h - 1]], axis=0))
        scores, lhs = lax.optimization_barrier((scores, lhs))
        received.append(lax.all_to_all(scores, "orient", 0, 0, tiled=True))
    pieces = jnp.concatenate(received, axis=1).reshape(orient_count, share_rows, tile_width)

    def merge(former, latter):
        return (
            jnp.maximum(former[0], latter[0]),
            jnp.maximum(jnp.minimum(former[0], latter[0]), jnp.maximum(former[1], latter[1])),
            former[2] + latter[2],
            former[3] + latter[3],
        )

    lowest = jnp.float32(-jnp.inf)
    top, second, total, squares = lax.reduce(
        (pieces, jnp.full_like(pieces, lowest), pieces, pieces * pieces),
        (lowest, lowest, jnp.float32(0.0), jnp.float32(0.0)),
        merge,
        (0,),
    )
    mean_map = total / orient_count
    variance = squares / orient_count - mean_map * mean_map
    return (top, second, mean_map, variance)


def solution(mesh):
    placed = (P("tile", None), P("orient", "tile", None), P(), P("tile"))
    return jax.shard_map(
        per_device,
        mesh=mesh,
        in_specs=placed,
        out_specs=(
            P(("tile", "orient"), None),
            P(("tile", "orient"), None),
            P(("tile", "orient"), None),
            P(("tile", "orient"), None),
        ),
        check_vma=False,
    )
```

```python
import math

import numpy as np
import jax
import jax.numpy as jnp
from jax import lax
from jax.sharding import PartitionSpec as P

TPL = 256


WAVELENGTH = 0.0197
AMPLITUDE = 0.07
mode = lax.Precision.HIGH


def padded(shard, sides, width):
    for axis, dim in sides:
        size, length = (lax.axis_size(axis), shard.shape[dim])
        up = [(i, (i + 1) % size) for i in range(size - 1)]
        down = [(j, i) for i, j in up]
        last = lax.slice_in_dim(shard, length - width, length, axis=dim)
        initial = lax.slice_in_dim(shard, 0, width, axis=dim)
        before = lax.ppermute(last, axis, up)
        after = lax.ppermute(initial, axis, down)
        shard = jnp.concatenate([before, shard, after], axis=dim)
    return shard


def product(former, latter):
    return jnp.dot(former, latter, precision=mode, preferred_element_type=jnp.float32)


def tables(tile_width, margin, extent):
    n = tile_width + 2 * margin
    h = n // 2 + 1
    idx = np.arange(n)
    angles = 2.0 * np.pi * ((idx[:, None] * idx[None, :]) % n) / n
    cos, sin = np.cos(angles), np.sin(angles)
    left = np.concatenate([cos[:h], sin[1:h - 1]], axis=0)
    left_t = left[:, :extent]
    window_cols = slice(margin, margin + tile_width)
    right_w = np.concatenate([cos[window_cols, :h], sin[window_cols, 1:h - 1]], axis=1)
    right_t = np.concatenate([cos[:extent, :h], sin[:extent, 1:h - 1]], axis=1)
    mirror = np.concatenate([np.arange(h), n - np.arange(1, h - 1)])
    back = np.concatenate([cos[mirror, :tile_width], sin[mirror, :tile_width]], axis=1)
    weight = np.full(h, 2.0)
    weight[0] = 1.0
    weight[-1] = 1.0
    final = np.concatenate(
        [cos[:tile_width, :h] * weight, -2.0 * sin[:tile_width, 1:h - 1]], axis=1
    ) / (n * n)
    as32 = lambda a: jnp.asarray(a.astype(np.float32))
    return tuple(as32(a) for a in (left, left_t, right_w, right_t, back, final))


def per_device(micrograph, templates, defocus_values, defocus_group):
    tile_rows, tile_width = micrograph.shape
    margin = TPL // 2
    n = tile_width + 2 * margin
    h = n // 2 + 1
    tile_count = lax.axis_size("tile")
    pixel_count = float(tile_rows * tile_width * tile_count)
    own_rows, tpl_width = templates.shape[1], templates.shape[2]
    halo = padded(micrograph, (("tile", 0),), margin)
    def lane_fold(columns):
        return sum(columns[i:i + tpl_width] for i in range(0, tile_width, tpl_width))[None, :]

    sum_row = lane_fold(jnp.sum(micrograph, axis=0))
    square_row = lane_fold(jnp.sum(micrograph * micrograph, axis=0))
    payload = jnp.concatenate([templates[0], sum_row, square_row], axis=0)
    everything = lax.all_gather(payload, "tile")
    gathered = everything[:, :own_rows].reshape(tile_count * own_rows, tpl_width)
    ones = jnp.ones((tpl_width, tpl_width), jnp.float32)

    def lane_total(rows):
        return jnp.dot(
            jnp.sum(rows, axis=0, keepdims=True), ones,
            precision=lax.Precision.HIGHEST, preferred_element_type=jnp.float32,
        )

    centre = lane_total(everything[:, own_rows]) / pixel_count
    spread = jnp.sqrt(lane_total(everything[:, own_rows + 1]) / pixel_count - centre * centre + 1e-05)
    reps = tile_width // tpl_width
    centre, spread = jnp.tile(centre, (1, reps)), jnp.tile(spread, (1, reps))
    tile_index = lax.axis_index("tile")
    row_ids = lax.broadcasted_iota(jnp.int32, (n, 1), 0)
    valid = ((row_ids >= margin) | (tile_index > 0)) & (
        (row_ids < margin + tile_rows) | (tile_index < tile_count - 1)
    )
    rows_ext = jnp.where(valid, (halo - centre) / spread, 0.0)
    extent = gathered.shape[0]
    left, left_t, right_w, right_t, back, final = tables(tile_width, margin, extent)

    tpl_count = float(gathered.shape[0] * gathered.shape[1])
    centred = gathered - lane_total(gathered) / tpl_count
    root_mean = jnp.sqrt(lane_total(centred * centred) / tpl_count + 1e-06)
    normed = centred / (root_mean * TPL)

    edge_rows, edge_cols = ((1, 1), (0, 0)), ((0, 0), (1, 1))

    def halves(packed):
        return packed[:h], jnp.pad(packed[h:], edge_rows)

    def direct(ga, gb):
        ga_s, gb_s = jnp.pad(ga[:, h:], edge_cols), jnp.pad(gb[:, h:], edge_cols)
        return ga[:, :h] - gb_s, -(ga_s + gb[:, :h])

    def mirrored(ga, gb):
        return ga[:, 1:h - 1] + gb[:, h:], ga[:, h:] - gb[:, 1:h - 1]

    window_parts = halves(product(product(left, rows_ext), right_w))
    template_parts = halves(product(product(left_t, normed), right_t))

    positions = lax.iota(jnp.int32, n)
    signed_freq = (
        jnp.where(positions < n // 2, positions, positions - n).astype(jnp.float32) / n
    )
    packed_freq = jnp.where(positions < h, positions, positions - (h - 1)).astype(jnp.float32) / n
    group_ids = lax.iota(jnp.int32, defocus_values.shape[0])
    defocus = jnp.sum(jnp.where(group_ids == defocus_group[0], defocus_values, 0.0))
    scale = math.pi * WAVELENGTH * defocus
    row_phase = scale * signed_freq[:h, None] ** 2
    col_phase = scale * packed_freq[None, :] ** 2
    sin_r, cos_r = jnp.sin(row_phase), jnp.cos(row_phase)
    sin_c, cos_c = jnp.sin(col_phase), jnp.cos(col_phase)
    weight_sin = math.sqrt(1.0 - AMPLITUDE * AMPLITUDE)
    col_u = weight_sin * cos_c - AMPLITUDE * sin_c
    col_v = weight_sin * sin_c + AMPLITUDE * cos_c
    contrast = -(sin_r * col_u + cos_r * col_v)
    def multiply(form, weight):
        spec_real, spec_imag = form(*window_parts)
        template_real, template_imag = form(*template_parts)
        return (
            (spec_real * template_real + spec_imag * template_imag) * weight,
            (spec_imag * template_real - spec_real * template_imag) * weight,
        )

    real_d, imag_d = multiply(direct, contrast[:, :h])
    real_m, imag_m = multiply(mirrored, contrast[:, h:])
    lhs = jnp.concatenate(
        [jnp.concatenate([real_d, real_m], axis=1), jnp.concatenate([imag_d, imag_m], axis=1)],
        axis=0,
    )
    inner = product(lhs, back)
    pr_c, pr_s = inner[:h, :tile_width], inner[:h, tile_width:]
    pi_c, pi_s = inner[h:, :tile_width], inner[h:, tile_width:]
    back_real = pr_c - pi_s
    back_imag = pr_s + pi_c
    scores = product(final, jnp.concatenate([back_real, back_imag[1:h - 1]], axis=0))

    orient_count = lax.axis_size("orient")
    share_rows = tile_rows // orient_count
    pieces = lax.all_to_all(scores, "orient", 0, 0, tiled=True).reshape(
        orient_count, share_rows, tile_width
    )
    def merge(former, latter):
        return (
            jnp.maximum(former[0], latter[0]),
            jnp.maximum(jnp.minimum(former[0], latter[0]), jnp.maximum(former[1], latter[1])),
            former[2] + latter[2],
            former[3] + latter[3],
        )

    lowest = jnp.float32(-jnp.inf)
    top, second, total, squares = lax.reduce(
        (pieces, jnp.full_like(pieces, lowest), pieces, pieces * pieces),
        (lowest, lowest, jnp.float32(0.0), jnp.float32(0.0)),
        merge,
        (0,),
    )
    mean_map = total / orient_count
    variance = squares / orient_count - mean_map * mean_map
    return (top, second, mean_map, variance)


def solution(mesh):
    placed = (P("tile", None), P("orient", "tile", None), P(), P("tile"))
    return jax.shard_map(
        per_device,
        mesh=mesh,
        in_specs=placed,
        out_specs=(
            P(("tile", "orient"), None),
            P(("tile", "orient"), None),
            P(("tile", "orient"), None),
            P(("tile", "orient"), None),
        ),
        check_vma=False,
    )
```

```python
import math

import numpy as np
import jax
import jax.numpy as jnp
from jax import lax
from jax.sharding import PartitionSpec as P

TPL = 256


WAVELENGTH = 0.0197
AMPLITUDE = 0.07
mode = lax.Precision.HIGH


def padded(shard, sides, width):
    for axis, dim in sides:
        size, length = (lax.axis_size(axis), shard.shape[dim])
        up = [(i, (i + 1) % size) for i in range(size - 1)]
        down = [(j, i) for i, j in up]
        last = lax.slice_in_dim(shard, length - width, length, axis=dim)
        initial = lax.slice_in_dim(shard, 0, width, axis=dim)
        before = lax.ppermute(last, axis, up)
        after = lax.ppermute(initial, axis, down)
        shard = jnp.concatenate([before, shard, after], axis=dim)
    return shard


def product(former, latter):
    return jnp.dot(former, latter, precision=mode, preferred_element_type=jnp.float32)


def tables(tile_width, margin, extent):
    n = tile_width + 2 * margin
    h = n // 2 + 1
    idx = np.arange(n)
    angles = 2.0 * np.pi * ((idx[:, None] * idx[None, :]) % n) / n
    cos, sin = np.cos(angles), np.sin(angles)
    left = np.concatenate([cos[:h], sin[1:h - 1]], axis=0)
    left_t = left[:, :extent]
    window_cols = slice(margin, margin + tile_width)
    right_w = np.concatenate([cos[window_cols, :h], sin[window_cols, 1:h - 1]], axis=1)
    right_t = np.concatenate([cos[:extent, :h], sin[:extent, 1:h - 1]], axis=1)
    mirror = np.concatenate([np.arange(h), n - np.arange(1, h - 1)])
    back = np.concatenate([cos[mirror, :tile_width], sin[mirror, :tile_width]], axis=1)
    weight = np.full(h, 2.0)
    weight[0] = 1.0
    weight[-1] = 1.0
    final = np.concatenate(
        [cos[:tile_width, :h] * weight, -2.0 * sin[:tile_width, 1:h - 1]], axis=1
    ) / (n * n)
    as32 = lambda a: jnp.asarray(a.astype(np.float32))
    return tuple(as32(a) for a in (left, left_t, right_w, right_t, back, final))


def per_device(micrograph, templates, defocus_values, defocus_group):
    tile_rows, tile_width = micrograph.shape
    margin = TPL // 2
    n = tile_width + 2 * margin
    h = n // 2 + 1
    tile_count = lax.axis_size("tile")
    pixel_count = float(tile_rows * tile_width * tile_count)
    own_rows, tpl_width = templates.shape[1], templates.shape[2]
    halo = padded(micrograph, (("tile", 0),), margin)
    def lane_fold(columns):
        return sum(columns[i:i + tpl_width] for i in range(0, tile_width, tpl_width))[None, :]

    sum_row = lane_fold(jnp.sum(micrograph, axis=0))
    square_row = lane_fold(jnp.sum(micrograph * micrograph, axis=0))
    payload = jnp.concatenate([templates[0], sum_row, square_row], axis=0)
    everything = lax.all_gather(payload, "tile")
    gathered = everything[:, :own_rows].reshape(tile_count * own_rows, tpl_width)
    ones = jnp.ones((tpl_width, tpl_width), jnp.float32)

    def lane_total(rows):
        return jnp.dot(
            jnp.sum(rows, axis=0, keepdims=True), ones,
            precision=lax.Precision.HIGHEST, preferred_element_type=jnp.float32,
        )

    centre = lane_total(everything[:, own_rows]) / pixel_count
    spread = jnp.sqrt(lane_total(everything[:, own_rows + 1]) / pixel_count - centre * centre + 1e-05)
    reps = tile_width // tpl_width
    centre, spread = jnp.tile(centre, (1, reps)), jnp.tile(spread, (1, reps))
    tile_index = lax.axis_index("tile")
    row_ids = lax.broadcasted_iota(jnp.int32, (n, 1), 0)
    valid = ((row_ids >= margin) | (tile_index > 0)) & (
        (row_ids < margin + tile_rows) | (tile_index < tile_count - 1)
    )
    rows_ext = jnp.where(valid, (halo - centre) / spread, 0.0)
    extent = gathered.shape[0]
    left, left_t, right_w, right_t, back, final = tables(tile_width, margin, extent)

    tpl_count = float(gathered.shape[0] * gathered.shape[1])
    centred = gathered - lane_total(gathered) / tpl_count
    root_mean = jnp.sqrt(lane_total(centred * centred) / tpl_count + 1e-06)
    normed = centred / (root_mean * TPL)

    edge_rows, edge_cols = ((1, 1), (0, 0)), ((0, 0), (1, 1))

    def halves(packed):
        return packed[:h], jnp.pad(packed[h:], edge_rows)

    def direct(ga, gb):
        ga_s, gb_s = jnp.pad(ga[:, h:], edge_cols), jnp.pad(gb[:, h:], edge_cols)
        return ga[:, :h] - gb_s, -(ga_s + gb[:, :h])

    def mirrored(ga, gb):
        return ga[:, 1:h - 1] + gb[:, h:], ga[:, h:] - gb[:, 1:h - 1]

    window_parts = halves(product(product(left, rows_ext), right_w))
    template_parts = halves(product(product(left_t, normed), right_t))

    positions = lax.iota(jnp.int32, n)
    signed_freq = (
        jnp.where(positions < n // 2, positions, positions - n).astype(jnp.float32) / n
    )
    packed_freq = jnp.where(positions < h, positions, positions - (h - 1)).astype(jnp.float32) / n
    groups = defocus_values.shape[0]
    group = defocus_group[0]
    pick_cols = lax.broadcasted_iota(jnp.int32, (groups, n), 0) == group
    defocus_cols = jnp.sum(jnp.where(pick_cols, defocus_values[:, None], 0.0), axis=0)[None, :]
    pick_rows = lax.broadcasted_iota(jnp.int32, (h, groups), 1) == group
    defocus_rows = jnp.sum(jnp.where(pick_rows, defocus_values[None, :], 0.0), axis=1)[:, None]
    phase_unit = math.pi * WAVELENGTH
    row_phase = phase_unit * defocus_rows * signed_freq[:h, None] ** 2
    col_phase = phase_unit * defocus_cols * packed_freq[None, :] ** 2
    sin_r, cos_r = jnp.sin(row_phase), jnp.cos(row_phase)
    sin_c, cos_c = jnp.sin(col_phase), jnp.cos(col_phase)
    weight_sin = math.sqrt(1.0 - AMPLITUDE * AMPLITUDE)
    col_u = weight_sin * cos_c - AMPLITUDE * sin_c
    col_v = weight_sin * sin_c + AMPLITUDE * cos_c
    contrast = -(sin_r * col_u + cos_r * col_v)
    def multiply(form, weight):
        spec_real, spec_imag = form(*window_parts)
        template_real, template_imag = form(*template_parts)
        return (
            (spec_real * template_real + spec_imag * template_imag) * weight,
            (spec_imag * template_real - spec_real * template_imag) * weight,
        )

    real_d, imag_d = multiply(direct, contrast[:, :h])
    real_m, imag_m = multiply(mirrored, contrast[:, h:])
    lhs = jnp.concatenate(
        [jnp.concatenate([real_d, real_m], axis=1), jnp.concatenate([imag_d, imag_m], axis=1)],
        axis=0,
    )
    inner = product(lhs, back)
    pr_c, pr_s = inner[:h, :tile_width], inner[:h, tile_width:]
    pi_c, pi_s = inner[h:, :tile_width], inner[h:, tile_width:]
    back_real = pr_c - pi_s
    back_imag = pr_s + pi_c
    scores = product(final, jnp.concatenate([back_real, back_imag[1:h - 1]], axis=0))

    orient_count = lax.axis_size("orient")
    share_rows = tile_rows // orient_count
    pieces = lax.all_to_all(scores, "orient", 0, 0, tiled=True).reshape(
        orient_count, share_rows, tile_width
    )
    def merge(former, latter):
        return (
            jnp.maximum(former[0], latter[0]),
            jnp.maximum(jnp.minimum(former[0], latter[0]), jnp.maximum(former[1], latter[1])),
            former[2] + latter[2],
            former[3] + latter[3],
        )

    lowest = jnp.float32(-jnp.inf)
    top, second, total, squares = lax.reduce(
        (pieces, jnp.full_like(pieces, lowest), pieces, pieces * pieces),
        (lowest, lowest, jnp.float32(0.0), jnp.float32(0.0)),
        merge,
        (0,),
    )
    mean_map = total / orient_count
    variance = squares / orient_count - mean_map * mean_map
    return (top, second, mean_map, variance)


def solution(mesh):
    placed = (P("tile", None), P("orient", "tile", None), P(), P("tile"))
    return jax.shard_map(
        per_device,
        mesh=mesh,
        in_specs=placed,
        out_specs=(
            P(("tile", "orient"), None),
            P(("tile", "orient"), None),
            P(("tile", "orient"), None),
            P(("tile", "orient"), None),
        ),
        check_vma=False,
    )
```

```python
import math

import numpy as np
import jax
import jax.numpy as jnp
from jax import lax
from jax.sharding import PartitionSpec as P

TPL = 256


WAVELENGTH = 0.0197
AMPLITUDE = 0.07
mode = lax.Precision.HIGH


def padded(shard, sides, width):
    for axis, dim in sides:
        size, length = (lax.axis_size(axis), shard.shape[dim])
        up = [(i, (i + 1) % size) for i in range(size - 1)]
        down = [(j, i) for i, j in up]
        last = lax.slice_in_dim(shard, length - width, length, axis=dim)
        initial = lax.slice_in_dim(shard, 0, width, axis=dim)
        before = lax.ppermute(last, axis, up)
        after = lax.ppermute(initial, axis, down)
        shard = jnp.concatenate([before, shard, after], axis=dim)
    return shard


def product(former, latter):
    return jnp.dot(former, latter, precision=mode, preferred_element_type=jnp.float32)


def tables(tile_width, margin, extent):
    n = tile_width + 2 * margin
    h = n // 2 + 1
    idx = np.arange(n)
    angles = 2.0 * np.pi * ((idx[:, None] * idx[None, :]) % n) / n
    cos, sin = np.cos(angles), np.sin(angles)
    left = np.concatenate([cos[:h], sin[1:h - 1]], axis=0)
    left_t = left[:, :extent]
    window_cols = slice(margin, margin + tile_width)
    right_w = np.concatenate([cos[window_cols, :h], sin[window_cols, 1:h - 1]], axis=1)
    right_t = np.concatenate([cos[:extent, :h], sin[:extent, 1:h - 1]], axis=1)
    mirror = np.concatenate([np.arange(h), n - np.arange(1, h - 1)])
    back = np.concatenate([cos[mirror, :tile_width], sin[mirror, :tile_width]], axis=1)
    weight = np.full(h, 2.0)
    weight[0] = 1.0
    weight[-1] = 1.0
    final = np.concatenate(
        [cos[:tile_width, :h] * weight, -2.0 * sin[:tile_width, 1:h - 1]], axis=1
    ) / (n * n)
    as32 = lambda a: jnp.asarray(a.astype(np.float32))
    return tuple(as32(a) for a in (left, left_t, right_w, right_t, back, final))


def per_device(micrograph, templates, defocus_values, defocus_group):
    tile_rows, tile_width = micrograph.shape
    margin = TPL // 2
    n = tile_width + 2 * margin
    h = n // 2 + 1
    tile_count = lax.axis_size("tile")
    pixel_count = float(tile_rows * tile_width * tile_count)
    own_rows, tpl_width = templates.shape[1], templates.shape[2]
    halo = padded(micrograph, (("tile", 0),), margin)
    def lane_fold(columns):
        return sum(columns[i:i + tpl_width] for i in range(0, tile_width, tpl_width))[None, :]

    sum_row = lane_fold(jnp.sum(micrograph, axis=0))
    square_row = lane_fold(jnp.sum(micrograph * micrograph, axis=0))
    payload = jnp.concatenate([templates[0], sum_row, square_row], axis=0)
    everything = lax.all_gather(payload, "tile")
    defocus_values, defocus_group, everything = lax.optimization_barrier(
        (defocus_values, defocus_group, everything)
    )
    gathered = everything[:, :own_rows].reshape(tile_count * own_rows, tpl_width)
    ones = jnp.ones((tpl_width, tpl_width), jnp.float32)

    def lane_total(rows):
        return jnp.dot(
            jnp.sum(rows, axis=0, keepdims=True), ones,
            precision=lax.Precision.HIGHEST, preferred_element_type=jnp.float32,
        )

    centre = lane_total(everything[:, own_rows]) / pixel_count
    spread = jnp.sqrt(lane_total(everything[:, own_rows + 1]) / pixel_count - centre * centre + 1e-05)
    reps = tile_width // tpl_width
    centre, spread = jnp.tile(centre, (1, reps)), jnp.tile(spread, (1, reps))
    tile_index = lax.axis_index("tile")
    row_ids = lax.broadcasted_iota(jnp.int32, (n, 1), 0)
    valid = ((row_ids >= margin) | (tile_index > 0)) & (
        (row_ids < margin + tile_rows) | (tile_index < tile_count - 1)
    )
    rows_ext = jnp.where(valid, (halo - centre) / spread, 0.0)
    extent = gathered.shape[0]
    left, left_t, right_w, right_t, back, final = tables(tile_width, margin, extent)

    tpl_count = float(gathered.shape[0] * gathered.shape[1])
    centred = gathered - lane_total(gathered) / tpl_count
    root_mean = jnp.sqrt(lane_total(centred * centred) / tpl_count + 1e-06)
    normed = centred / (root_mean * TPL)

    edge_rows, edge_cols = ((1, 1), (0, 0)), ((0, 0), (1, 1))

    def halves(packed):
        return packed[:h], jnp.pad(packed[h:], edge_rows)

    def direct(ga, gb):
        ga_s, gb_s = jnp.pad(ga[:, h:], edge_cols), jnp.pad(gb[:, h:], edge_cols)
        return ga[:, :h] - gb_s, -(ga_s + gb[:, :h])

    def mirrored(ga, gb):
        return ga[:, 1:h - 1] + gb[:, h:], ga[:, h:] - gb[:, 1:h - 1]

    window_parts = halves(product(product(left, rows_ext), right_w))
    template_parts = halves(product(product(left_t, normed), right_t))

    positions = lax.iota(jnp.int32, n)
    signed_freq = (
        jnp.where(positions < n // 2, positions, positions - n).astype(jnp.float32) / n
    )
    packed_freq = jnp.where(positions < h, positions, positions - (h - 1)).astype(jnp.float32) / n
    groups = defocus_values.shape[0]
    group = defocus_group[0]
    pick_cols = lax.broadcasted_iota(jnp.int32, (groups, n), 0) == group
    defocus_cols = jnp.sum(jnp.where(pick_cols, defocus_values[:, None], 0.0), axis=0)[None, :]
    pick_rows = lax.broadcasted_iota(jnp.int32, (h, groups), 1) == group
    defocus_rows = jnp.sum(jnp.where(pick_rows, defocus_values[None, :], 0.0), axis=1)[:, None]
    phase_unit = math.pi * WAVELENGTH
    row_phase = phase_unit * defocus_rows * signed_freq[:h, None] ** 2
    col_phase = phase_unit * defocus_cols * packed_freq[None, :] ** 2
    sin_r, cos_r = jnp.sin(row_phase), jnp.cos(row_phase)
    sin_c, cos_c = jnp.sin(col_phase), jnp.cos(col_phase)
    weight_sin = math.sqrt(1.0 - AMPLITUDE * AMPLITUDE)
    col_u = weight_sin * cos_c - AMPLITUDE * sin_c
    col_v = weight_sin * sin_c + AMPLITUDE * cos_c
    contrast = -(sin_r * col_u + cos_r * col_v)
    def multiply(form, weight):
        spec_real, spec_imag = form(*window_parts)
        template_real, template_imag = form(*template_parts)
        return (
            (spec_real * template_real + spec_imag * template_imag) * weight,
            (spec_imag * template_real - spec_real * template_imag) * weight,
        )

    real_d, imag_d = multiply(direct, contrast[:, :h])
    real_m, imag_m = multiply(mirrored, contrast[:, h:])
    lhs = jnp.concatenate(
        [jnp.concatenate([real_d, real_m], axis=1), jnp.concatenate([imag_d, imag_m], axis=1)],
        axis=0,
    )
    inner = product(lhs, back)
    pr_c, pr_s = inner[:h, :tile_width], inner[:h, tile_width:]
    pi_c, pi_s = inner[h:, :tile_width], inner[h:, tile_width:]
    back_real = pr_c - pi_s
    back_imag = pr_s + pi_c
    scores = product(final, jnp.concatenate([back_real, back_imag[1:h - 1]], axis=0))

    orient_count = lax.axis_size("orient")
    share_rows = tile_rows // orient_count
    pieces = lax.all_to_all(scores, "orient", 0, 0, tiled=True).reshape(
        orient_count, share_rows, tile_width
    )
    def merge(former, latter):
        return (
            jnp.maximum(former[0], latter[0]),
            jnp.maximum(jnp.minimum(former[0], latter[0]), jnp.maximum(former[1], latter[1])),
            former[2] + latter[2],
            former[3] + latter[3],
        )

    lowest = jnp.float32(-jnp.inf)
    top, second, total, squares = lax.reduce(
        (pieces, jnp.full_like(pieces, lowest), pieces, pieces * pieces),
        (lowest, lowest, jnp.float32(0.0), jnp.float32(0.0)),
        merge,
        (0,),
    )
    mean_map = total / orient_count
    variance = squares / orient_count - mean_map * mean_map
    return (top, second, mean_map, variance)


def solution(mesh):
    placed = (P("tile", None), P("orient", "tile", None), P(), P("tile"))
    return jax.shard_map(
        per_device,
        mesh=mesh,
        in_specs=placed,
        out_specs=(
            P(("tile", "orient"), None),
            P(("tile", "orient"), None),
            P(("tile", "orient"), None),
            P(("tile", "orient"), None),
        ),
        check_vma=False,
    )
```

```python
import math

import numpy as np
import jax
import jax.numpy as jnp
from jax import lax
from jax.sharding import PartitionSpec as P

TPL = 256


WAVELENGTH = 0.0197
AMPLITUDE = 0.07
mode = lax.Precision.HIGH


def padded(shard, sides, width):
    for axis, dim in sides:
        size, length = (lax.axis_size(axis), shard.shape[dim])
        up = [(i, (i + 1) % size) for i in range(size - 1)]
        down = [(j, i) for i, j in up]
        last = lax.slice_in_dim(shard, length - width, length, axis=dim)
        initial = lax.slice_in_dim(shard, 0, width, axis=dim)
        before = lax.ppermute(last, axis, up)
        after = lax.ppermute(initial, axis, down)
        shard = jnp.concatenate([before, shard, after], axis=dim)
    return shard


def product(former, latter):
    return jnp.dot(former, latter, precision=mode, preferred_element_type=jnp.float32)


def tables(tile_width, margin, extent):
    n = tile_width + 2 * margin
    h = n // 2 + 1
    idx = np.arange(n)
    angles = 2.0 * np.pi * ((idx[:, None] * idx[None, :]) % n) / n
    cos, sin = np.cos(angles), np.sin(angles)
    left = np.concatenate([cos[:h], sin[1:h - 1]], axis=0)
    left_t = left[:, :extent]
    window_cols = slice(margin, margin + tile_width)
    right_w = np.concatenate([cos[window_cols, :h], sin[window_cols, 1:h - 1]], axis=1)
    right_t = np.concatenate([cos[:extent, :h], sin[:extent, 1:h - 1]], axis=1)
    mirror = np.concatenate([np.arange(h), n - np.arange(1, h - 1)])
    back = np.concatenate([cos[mirror, :tile_width], sin[mirror, :tile_width]], axis=1)
    weight = np.full(h, 2.0)
    weight[0] = 1.0
    weight[-1] = 1.0
    final = np.concatenate(
        [cos[:tile_width, :h] * weight, -2.0 * sin[:tile_width, 1:h - 1]], axis=1
    ) / (n * n)
    as32 = lambda a: jnp.asarray(a.astype(np.float32))
    return tuple(as32(a) for a in (left, left_t, right_w, right_t, back, final))


def per_device(micrograph, templates, defocus_values, defocus_group):
    tile_rows, tile_width = micrograph.shape
    margin = TPL // 2
    n = tile_width + 2 * margin
    h = n // 2 + 1
    tile_count = lax.axis_size("tile")
    pixel_count = float(tile_rows * tile_width * tile_count)
    own_rows, tpl_width = templates.shape[1], templates.shape[2]
    halo = padded(micrograph, (("tile", 0),), margin)
    def lane_fold(columns):
        return sum(columns[i:i + tpl_width] for i in range(0, tile_width, tpl_width))[None, :]

    sum_row = lane_fold(jnp.sum(micrograph, axis=0))
    square_row = lane_fold(jnp.sum(micrograph * micrograph, axis=0))
    payload = jnp.concatenate([templates[0], sum_row, square_row], axis=0)
    everything = lax.all_gather(payload, "tile")
    defocus_values, defocus_group, everything = lax.optimization_barrier(
        (defocus_values, defocus_group, everything)
    )
    gathered = everything[:, :own_rows].reshape(tile_count * own_rows, tpl_width)
    ones = jnp.ones((tpl_width, tpl_width), jnp.float32)

    def lane_total(rows):
        return jnp.dot(
            jnp.sum(rows, axis=0, keepdims=True), ones,
            precision=lax.Precision.HIGHEST, preferred_element_type=jnp.float32,
        )

    centre = lane_total(everything[:, own_rows]) / pixel_count
    spread = jnp.sqrt(lane_total(everything[:, own_rows + 1]) / pixel_count - centre * centre + 1e-05)
    reps = tile_width // tpl_width
    centre, spread = jnp.tile(centre, (1, reps)), jnp.tile(spread, (1, reps))
    tile_index = lax.axis_index("tile")
    row_ids = lax.broadcasted_iota(jnp.int32, (n, 1), 0)
    valid = ((row_ids >= margin) | (tile_index > 0)) & (
        (row_ids < margin + tile_rows) | (tile_index < tile_count - 1)
    )
    rows_ext = jnp.where(valid, (halo - centre) / spread, 0.0)
    extent = gathered.shape[0]
    left, left_t, right_w, right_t, back, final = tables(tile_width, margin, extent)

    tpl_count = float(gathered.shape[0] * gathered.shape[1])
    centred = gathered - lane_total(gathered) / tpl_count
    root_mean = jnp.sqrt(lane_total(centred * centred) / tpl_count + 1e-06)
    normed = centred / (root_mean * TPL)

    edge_rows, edge_cols = ((1, 1), (0, 0)), ((0, 0), (1, 1))

    def halves(packed):
        return packed[:h], jnp.pad(packed[h:], edge_rows)

    def direct(ga, gb):
        ga_s, gb_s = jnp.pad(ga[:, h:], edge_cols), jnp.pad(gb[:, h:], edge_cols)
        return ga[:, :h] - gb_s, -(ga_s + gb[:, :h])

    def mirrored(ga, gb):
        return ga[:, 1:h - 1] + gb[:, h:], ga[:, h:] - gb[:, 1:h - 1]

    window_parts = halves(product(product(left, rows_ext), right_w))
    template_parts = halves(product(product(left_t, normed), right_t))

    positions = lax.iota(jnp.int32, n)
    signed_freq = (
        jnp.where(positions < n // 2, positions, positions - n).astype(jnp.float32) / n
    )
    packed_freq = jnp.where(positions < h, positions, positions - (h - 1)).astype(jnp.float32) / n
    groups = defocus_values.shape[0]
    group = defocus_group[0]
    pick_cols = lax.broadcasted_iota(jnp.int32, (groups, n), 0) == group
    defocus_cols = jnp.sum(jnp.where(pick_cols, defocus_values[:, None], 0.0), axis=0)[None, :]
    pick_rows = lax.broadcasted_iota(jnp.int32, (h, groups), 1) == group
    defocus_rows = jnp.sum(jnp.where(pick_rows, defocus_values[None, :], 0.0), axis=1)[:, None]
    phase_unit = math.pi * WAVELENGTH
    row_phase = phase_unit * defocus_rows * signed_freq[:h, None] ** 2
    col_phase = phase_unit * defocus_cols * packed_freq[None, :] ** 2
    sin_r, cos_r = jnp.sin(row_phase), jnp.cos(row_phase)
    sin_c, cos_c = jnp.sin(col_phase), jnp.cos(col_phase)
    weight_sin = math.sqrt(1.0 - AMPLITUDE * AMPLITUDE)
    col_u = weight_sin * cos_c - AMPLITUDE * sin_c
    col_v = weight_sin * sin_c + AMPLITUDE * cos_c
    contrast = -(sin_r * col_u + cos_r * col_v)
    def multiply(form, weight):
        spec_real, spec_imag = form(*window_parts)
        template_real, template_imag = form(*template_parts)
        return (
            (spec_real * template_real + spec_imag * template_imag) * weight,
            (spec_imag * template_real - spec_real * template_imag) * weight,
        )

    real_d, imag_d = multiply(direct, contrast[:, :h])
    real_m, imag_m = multiply(mirrored, contrast[:, h:])
    lhs = jnp.concatenate(
        [jnp.concatenate([real_d, real_m], axis=1), jnp.concatenate([imag_d, imag_m], axis=1)],
        axis=0,
    )
    inner = product(lhs, back)
    pr_c, pr_s = inner[:h, :tile_width], inner[:h, tile_width:]
    pi_c, pi_s = inner[h:, :tile_width], inner[h:, tile_width:]
    back_real = pr_c - pi_s
    back_imag = pr_s + pi_c
    split = h - 1
    slot = lax.broadcasted_iota(jnp.int32, (split, 1), 0) == 0
    tail = jnp.where(slot, back_real[split:], jnp.pad(back_imag[1:split], ((1, 0), (0, 0))))
    scores = product(final, jnp.concatenate([back_real[:split], tail], axis=0))

    orient_count = lax.axis_size("orient")
    share_rows = tile_rows // orient_count
    pieces = lax.all_to_all(scores, "orient", 0, 0, tiled=True).reshape(
        orient_count, share_rows, tile_width
    )
    def merge(former, latter):
        return (
            jnp.maximum(former[0], latter[0]),
            jnp.maximum(jnp.minimum(former[0], latter[0]), jnp.maximum(former[1], latter[1])),
            former[2] + latter[2],
            former[3] + latter[3],
        )

    lowest = jnp.float32(-jnp.inf)
    top, second, total, squares = lax.reduce(
        (pieces, jnp.full_like(pieces, lowest), pieces, pieces * pieces),
        (lowest, lowest, jnp.float32(0.0), jnp.float32(0.0)),
        merge,
        (0,),
    )
    mean_map = total / orient_count
    variance = squares / orient_count - mean_map * mean_map
    return (top, second, mean_map, variance)


def solution(mesh):
    placed = (P("tile", None), P("orient", "tile", None), P(), P("tile"))
    return jax.shard_map(
        per_device,
        mesh=mesh,
        in_specs=placed,
        out_specs=(
            P(("tile", "orient"), None),
            P(("tile", "orient"), None),
            P(("tile", "orient"), None),
            P(("tile", "orient"), None),
        ),
        check_vma=False,
    )
```

```python
import math

import numpy as np
import jax
import jax.numpy as jnp
from jax import lax
from jax.sharding import PartitionSpec as P

TPL = 256


WAVELENGTH = 0.0197
AMPLITUDE = 0.07
mode = lax.Precision.HIGH


def padded(shard, sides, width):
    for axis, dim in sides:
        size, length = (lax.axis_size(axis), shard.shape[dim])
        up = [(i, (i + 1) % size) for i in range(size - 1)]
        down = [(j, i) for i, j in up]
        last = lax.slice_in_dim(shard, length - width, length, axis=dim)
        initial = lax.slice_in_dim(shard, 0, width, axis=dim)
        before = lax.ppermute(last, axis, up)
        after = lax.ppermute(initial, axis, down)
        shard = jnp.concatenate([before, shard, after], axis=dim)
    return shard


def product(former, latter):
    return jnp.dot(former, latter, precision=mode, preferred_element_type=jnp.float32)


def tables(tile_width, margin, extent):
    n = tile_width + 2 * margin
    h = n // 2 + 1
    idx = np.arange(n)
    angles = 2.0 * np.pi * ((idx[:, None] * idx[None, :]) % n) / n
    cos, sin = np.cos(angles), np.sin(angles)
    left = np.concatenate([cos[:h], sin[1:h - 1]], axis=0)
    left_t = left[:, :extent]
    window_cols = slice(margin, margin + tile_width)
    right_w = np.concatenate([cos[window_cols, :h], sin[window_cols, 1:h - 1]], axis=1)
    right_t = np.concatenate([cos[:extent, :h], sin[:extent, 1:h - 1]], axis=1)
    mirror = np.concatenate([np.arange(h), n - np.arange(1, h - 1)])
    back = np.concatenate([cos[mirror, :tile_width], sin[mirror, :tile_width]], axis=1)
    weight = np.full(h, 2.0)
    weight[0] = 1.0
    weight[-1] = 1.0
    final = np.concatenate(
        [cos[:tile_width, :h] * weight, -2.0 * sin[:tile_width, 1:h - 1]], axis=1
    ) / (n * n)
    as32 = lambda a: jnp.asarray(a.astype(np.float32))
    return tuple(as32(a) for a in (left, left_t, right_w, right_t, back, final))


def per_device(micrograph, templates, defocus_values, defocus_group):
    tile_rows, tile_width = micrograph.shape
    margin = TPL // 2
    n = tile_width + 2 * margin
    h = n // 2 + 1
    tile_count = lax.axis_size("tile")
    pixel_count = float(tile_rows * tile_width * tile_count)
    own_rows, tpl_width = templates.shape[1], templates.shape[2]
    halo = padded(micrograph, (("tile", 0),), margin)
    def lane_fold(columns):
        return sum(columns[i:i + tpl_width] for i in range(0, tile_width, tpl_width))[None, :]

    sum_row = lane_fold(jnp.sum(micrograph, axis=0))
    square_row = lane_fold(jnp.sum(micrograph * micrograph, axis=0))
    payload = jnp.concatenate([templates[0], sum_row, square_row], axis=0)
    everything = lax.all_gather(payload, "tile")
    defocus_values, defocus_group, everything = lax.optimization_barrier(
        (defocus_values, defocus_group, everything)
    )
    gathered = everything[:, :own_rows].reshape(tile_count * own_rows, tpl_width)
    ones = jnp.ones((tpl_width, tpl_width), jnp.float32)

    def lane_total(rows):
        return jnp.dot(
            jnp.sum(rows, axis=0, keepdims=True), ones,
            precision=lax.Precision.HIGHEST, preferred_element_type=jnp.float32,
        )

    centre = lane_total(everything[:, own_rows]) / pixel_count
    spread = jnp.sqrt(lane_total(everything[:, own_rows + 1]) / pixel_count - centre * centre + 1e-05)
    reps = tile_width // tpl_width
    centre, spread = jnp.tile(centre, (1, reps)), jnp.tile(spread, (1, reps))
    tile_index = lax.axis_index("tile")
    row_ids = lax.broadcasted_iota(jnp.int32, (n, 1), 0)
    valid = ((row_ids >= margin) | (tile_index > 0)) & (
        (row_ids < margin + tile_rows) | (tile_index < tile_count - 1)
    )
    rows_ext = jnp.where(valid, (halo - centre) / spread, 0.0)
    extent = gathered.shape[0]
    left, left_t, right_w, right_t, back, final = tables(tile_width, margin, extent)

    tpl_count = float(gathered.shape[0] * gathered.shape[1])
    centred = gathered - lane_total(gathered) / tpl_count
    root_mean = jnp.sqrt(lane_total(centred * centred) / tpl_count + 1e-06)
    normed = centred / (root_mean * TPL)

    edge_rows, edge_cols = ((1, 1), (0, 0)), ((0, 0), (1, 1))

    def halves(packed):
        return packed[:h], jnp.pad(packed[h:], edge_rows)

    def direct(ga, gb):
        ga_s, gb_s = jnp.pad(ga[:, h:], edge_cols), jnp.pad(gb[:, h:], edge_cols)
        return ga[:, :h] - gb_s, -(ga_s + gb[:, :h])

    def mirrored(ga, gb):
        return ga[:, 1:h - 1] + gb[:, h:], ga[:, h:] - gb[:, 1:h - 1]

    window_rows = product(left, rows_ext)
    window_rows, normed = lax.optimization_barrier((window_rows, normed))
    window_parts = halves(product(window_rows, right_w))
    template_parts = halves(product(product(left_t, normed), right_t))

    positions = lax.iota(jnp.int32, n)
    signed_freq = (
        jnp.where(positions < n // 2, positions, positions - n).astype(jnp.float32) / n
    )
    packed_freq = jnp.where(positions < h, positions, positions - (h - 1)).astype(jnp.float32) / n
    groups = defocus_values.shape[0]
    group = defocus_group[0]
    pick_cols = lax.broadcasted_iota(jnp.int32, (groups, n), 0) == group
    defocus_cols = jnp.sum(jnp.where(pick_cols, defocus_values[:, None], 0.0), axis=0)[None, :]
    pick_rows = lax.broadcasted_iota(jnp.int32, (h, groups), 1) == group
    defocus_rows = jnp.sum(jnp.where(pick_rows, defocus_values[None, :], 0.0), axis=1)[:, None]
    phase_unit = math.pi * WAVELENGTH
    row_phase = phase_unit * defocus_rows * signed_freq[:h, None] ** 2
    col_phase = phase_unit * defocus_cols * packed_freq[None, :] ** 2
    sin_r, cos_r = jnp.sin(row_phase), jnp.cos(row_phase)
    sin_c, cos_c = jnp.sin(col_phase), jnp.cos(col_phase)
    weight_sin = math.sqrt(1.0 - AMPLITUDE * AMPLITUDE)
    col_u = weight_sin * cos_c - AMPLITUDE * sin_c
    col_v = weight_sin * sin_c + AMPLITUDE * cos_c
    contrast = -(sin_r * col_u + cos_r * col_v)
    def multiply(form, weight):
        spec_real, spec_imag = form(*window_parts)
        template_real, template_imag = form(*template_parts)
        return (
            (spec_real * template_real + spec_imag * template_imag) * weight,
            (spec_imag * template_real - spec_real * template_imag) * weight,
        )

    real_d, imag_d = multiply(direct, contrast[:, :h])
    real_m, imag_m = multiply(mirrored, contrast[:, h:])
    lhs = jnp.concatenate(
        [jnp.concatenate([real_d, real_m], axis=1), jnp.concatenate([imag_d, imag_m], axis=1)],
        axis=0,
    )
    inner = product(lhs, back)
    pr_c, pr_s = inner[:h, :tile_width], inner[:h, tile_width:]
    pi_c, pi_s = inner[h:, :tile_width], inner[h:, tile_width:]
    back_real = pr_c - pi_s
    back_imag = pr_s + pi_c
    scores = product(final, jnp.concatenate([back_real, back_imag[1:h - 1]], axis=0))

    orient_count = lax.axis_size("orient")
    share_rows = tile_rows // orient_count
    pieces = lax.all_to_all(scores, "orient", 0, 0, tiled=True).reshape(
        orient_count, share_rows, tile_width
    )
    def merge(former, latter):
        return (
            jnp.maximum(former[0], latter[0]),
            jnp.maximum(jnp.minimum(former[0], latter[0]), jnp.maximum(former[1], latter[1])),
            former[2] + latter[2],
            former[3] + latter[3],
        )

    lowest = jnp.float32(-jnp.inf)
    top, second, total, squares = lax.reduce(
        (pieces, jnp.full_like(pieces, lowest), pieces, pieces * pieces),
        (lowest, lowest, jnp.float32(0.0), jnp.float32(0.0)),
        merge,
        (0,),
    )
    mean_map = total / orient_count
    variance = squares / orient_count - mean_map * mean_map
    return (top, second, mean_map, variance)


def solution(mesh):
    placed = (P("tile", None), P("orient", "tile", None), P(), P("tile"))
    return jax.shard_map(
        per_device,
        mesh=mesh,
        in_specs=placed,
        out_specs=(
            P(("tile", "orient"), None),
            P(("tile", "orient"), None),
            P(("tile", "orient"), None),
            P(("tile", "orient"), None),
        ),
        check_vma=False,
    )
```

```python
import math

import numpy as np
import jax
import jax.numpy as jnp
from jax import lax
from jax.sharding import PartitionSpec as P

TPL = 256


WAVELENGTH = 0.0197
AMPLITUDE = 0.07
mode = lax.Precision.HIGH


def padded(shard, sides, width):
    for axis, dim in sides:
        size, length = (lax.axis_size(axis), shard.shape[dim])
        up = [(i, (i + 1) % size) for i in range(size - 1)]
        down = [(j, i) for i, j in up]
        last = lax.slice_in_dim(shard, length - width, length, axis=dim)
        initial = lax.slice_in_dim(shard, 0, width, axis=dim)
        before = lax.ppermute(last, axis, up)
        after = lax.ppermute(initial, axis, down)
        shard = jnp.concatenate([before, shard, after], axis=dim)
    return shard


def product(former, latter):
    return jnp.dot(former, latter, precision=mode, preferred_element_type=jnp.float32)


def tables(tile_width, margin, extent):
    n = tile_width + 2 * margin
    h = n // 2 + 1
    idx = np.arange(n)
    angles = 2.0 * np.pi * ((idx[:, None] * idx[None, :]) % n) / n
    cos, sin = np.cos(angles), np.sin(angles)
    left = np.concatenate([cos[:h], sin[1:h - 1]], axis=0)
    left_t = left[:, :extent]
    window_cols = slice(margin, margin + tile_width)
    right_w = np.concatenate([cos[window_cols, :h], sin[window_cols, 1:h - 1]], axis=1)
    right_t = np.concatenate([cos[:extent, :h], sin[:extent, 1:h - 1]], axis=1)
    mirror = np.concatenate([np.arange(h), n - np.arange(1, h - 1)])
    back = np.concatenate([cos[mirror, :tile_width], sin[mirror, :tile_width]], axis=1)
    weight = np.full(h, 2.0)
    weight[0] = 1.0
    weight[-1] = 1.0
    final = np.concatenate(
        [cos[:tile_width, :h] * weight, -2.0 * sin[:tile_width, 1:h - 1]], axis=1
    ) / (n * n)
    as32 = lambda a: jnp.asarray(a.astype(np.float32))
    return tuple(as32(a) for a in (left, left_t, right_w, right_t, back, final))


def per_device(micrograph, templates, defocus_values, defocus_group):
    tile_rows, tile_width = micrograph.shape
    margin = TPL // 2
    n = tile_width + 2 * margin
    h = n // 2 + 1
    tile_count = lax.axis_size("tile")
    pixel_count = float(tile_rows * tile_width * tile_count)
    own_rows, tpl_width = templates.shape[1], templates.shape[2]
    halo = padded(micrograph, (("tile", 0),), margin)
    def lane_fold(columns):
        return sum(columns[i:i + tpl_width] for i in range(0, tile_width, tpl_width))[None, :]

    sum_row = lane_fold(jnp.sum(micrograph, axis=0))
    square_row = lane_fold(jnp.sum(micrograph * micrograph, axis=0))
    payload = jnp.concatenate([templates[0], sum_row, square_row], axis=0)
    everything = lax.all_gather(payload, "tile")
    defocus_values, defocus_group, everything = lax.optimization_barrier(
        (defocus_values, defocus_group, everything)
    )
    gathered = everything[:, :own_rows].reshape(tile_count * own_rows, tpl_width)
    ones = jnp.ones((tpl_width, tpl_width), jnp.float32)

    def lane_total(rows):
        return jnp.dot(
            jnp.sum(rows, axis=0, keepdims=True), ones,
            precision=lax.Precision.HIGHEST, preferred_element_type=jnp.float32,
        )

    centre = lane_total(everything[:, own_rows]) / pixel_count
    spread = jnp.sqrt(lane_total(everything[:, own_rows + 1]) / pixel_count - centre * centre + 1e-05)
    reps = tile_width // tpl_width
    centre, spread = jnp.tile(centre, (1, reps)), jnp.tile(spread, (1, reps))
    tile_index = lax.axis_index("tile")
    row_ids = lax.broadcasted_iota(jnp.int32, (n, 1), 0)
    valid = ((row_ids >= margin) | (tile_index > 0)) & (
        (row_ids < margin + tile_rows) | (tile_index < tile_count - 1)
    )
    rows_ext = jnp.where(valid, (halo - centre) / spread, 0.0)
    extent = gathered.shape[0]
    left, left_t, right_w, right_t, back, final = tables(tile_width, margin, extent)

    tpl_count = float(gathered.shape[0] * gathered.shape[1])
    centred = gathered - lane_total(gathered) / tpl_count
    root_mean = jnp.sqrt(lane_total(centred * centred) / tpl_count + 1e-06)
    normed = centred / (root_mean * TPL)

    edge_rows, edge_cols = ((1, 1), (0, 0)), ((0, 0), (1, 1))

    def halves(packed):
        return packed[:h], jnp.pad(packed[h:], edge_rows)

    def direct(ga, gb):
        ga_s, gb_s = jnp.pad(ga[:, h:], edge_cols), jnp.pad(gb[:, h:], edge_cols)
        return ga[:, :h] - gb_s, -(ga_s + gb[:, :h])

    def mirrored(ga, gb):
        return ga[:, 1:h - 1] + gb[:, h:], ga[:, h:] - gb[:, 1:h - 1]

    window_rows = product(left, rows_ext)
    window_rows, normed = lax.optimization_barrier((window_rows, normed))
    template_rows = product(left_t, normed)
    template_rows, window_rows = lax.optimization_barrier((template_rows, window_rows))
    window_parts = halves(product(window_rows, right_w))
    template_parts = halves(product(template_rows, right_t))

    positions = lax.iota(jnp.int32, n)
    signed_freq = (
        jnp.where(positions < n // 2, positions, positions - n).astype(jnp.float32) / n
    )
    packed_freq = jnp.where(positions < h, positions, positions - (h - 1)).astype(jnp.float32) / n
    groups = defocus_values.shape[0]
    group = defocus_group[0]
    pick_cols = lax.broadcasted_iota(jnp.int32, (groups, n), 0) == group
    defocus_cols = jnp.sum(jnp.where(pick_cols, defocus_values[:, None], 0.0), axis=0)[None, :]
    pick_rows = lax.broadcasted_iota(jnp.int32, (h, groups), 1) == group
    defocus_rows = jnp.sum(jnp.where(pick_rows, defocus_values[None, :], 0.0), axis=1)[:, None]
    phase_unit = math.pi * WAVELENGTH
    row_phase = phase_unit * defocus_rows * signed_freq[:h, None] ** 2
    col_phase = phase_unit * defocus_cols * packed_freq[None, :] ** 2
    sin_r, cos_r = jnp.sin(row_phase), jnp.cos(row_phase)
    sin_c, cos_c = jnp.sin(col_phase), jnp.cos(col_phase)
    weight_sin = math.sqrt(1.0 - AMPLITUDE * AMPLITUDE)
    col_u = weight_sin * cos_c - AMPLITUDE * sin_c
    col_v = weight_sin * sin_c + AMPLITUDE * cos_c
    contrast = -(sin_r * col_u + cos_r * col_v)
    def multiply(form, weight):
        spec_real, spec_imag = form(*window_parts)
        template_real, template_imag = form(*template_parts)
        return (
            (spec_real * template_real + spec_imag * template_imag) * weight,
            (spec_imag * template_real - spec_real * template_imag) * weight,
        )

    real_d, imag_d = multiply(direct, contrast[:, :h])
    real_m, imag_m = multiply(mirrored, contrast[:, h:])
    lhs = jnp.concatenate(
        [jnp.concatenate([real_d, real_m], axis=1), jnp.concatenate([imag_d, imag_m], axis=1)],
        axis=0,
    )
    inner = product(lhs, back)
    pr_c, pr_s = inner[:h, :tile_width], inner[:h, tile_width:]
    pi_c, pi_s = inner[h:, :tile_width], inner[h:, tile_width:]
    back_real = pr_c - pi_s
    back_imag = pr_s + pi_c
    scores = product(final, jnp.concatenate([back_real, back_imag[1:h - 1]], axis=0))

    orient_count = lax.axis_size("orient")
    share_rows = tile_rows // orient_count
    pieces = lax.all_to_all(scores, "orient", 0, 0, tiled=True).reshape(
        orient_count, share_rows, tile_width
    )
    def merge(former, latter):
        return (
            jnp.maximum(former[0], latter[0]),
            jnp.maximum(jnp.minimum(former[0], latter[0]), jnp.maximum(former[1], latter[1])),
            former[2] + latter[2],
            former[3] + latter[3],
        )

    lowest = jnp.float32(-jnp.inf)
    top, second, total, squares = lax.reduce(
        (pieces, jnp.full_like(pieces, lowest), pieces, pieces * pieces),
        (lowest, lowest, jnp.float32(0.0), jnp.float32(0.0)),
        merge,
        (0,),
    )
    mean_map = total / orient_count
    variance = squares / orient_count - mean_map * mean_map
    return (top, second, mean_map, variance)


def solution(mesh):
    placed = (P("tile", None), P("orient", "tile", None), P(), P("tile"))
    return jax.shard_map(
        per_device,
        mesh=mesh,
        in_specs=placed,
        out_specs=(
            P(("tile", "orient"), None),
            P(("tile", "orient"), None),
            P(("tile", "orient"), None),
            P(("tile", "orient"), None),
        ),
        check_vma=False,
    )
```

```python
import math

import numpy as np
import jax
import jax.numpy as jnp
from jax import lax
from jax.sharding import PartitionSpec as P

TPL = 256


WAVELENGTH = 0.0197
AMPLITUDE = 0.07
mode = lax.Precision.HIGH


def padded(shard, sides, width):
    for axis, dim in sides:
        size, length = (lax.axis_size(axis), shard.shape[dim])
        up = [(i, (i + 1) % size) for i in range(size - 1)]
        down = [(j, i) for i, j in up]
        last = lax.slice_in_dim(shard, length - width, length, axis=dim)
        initial = lax.slice_in_dim(shard, 0, width, axis=dim)
        before = lax.ppermute(last, axis, up)
        after = lax.ppermute(initial, axis, down)
        shard = jnp.concatenate([before, shard, after], axis=dim)
    return shard


def product(former, latter):
    return jnp.dot(former, latter, precision=mode, preferred_element_type=jnp.float32)


def tables(tile_width, margin, extent):
    n = tile_width + 2 * margin
    h = n // 2 + 1
    idx = np.arange(n)
    angles = 2.0 * np.pi * ((idx[:, None] * idx[None, :]) % n) / n
    cos, sin = np.cos(angles), np.sin(angles)
    left = np.concatenate([cos[:h], sin[1:h - 1]], axis=0)
    left_t = left[:, :extent]
    window_cols = slice(margin, margin + tile_width)
    right_w = np.concatenate([cos[window_cols, :h], sin[window_cols, 1:h - 1]], axis=1)
    right_t = np.concatenate([cos[:extent, :h], sin[:extent, 1:h - 1]], axis=1)
    mirror = np.concatenate([np.arange(h), n - np.arange(1, h - 1)])
    back = np.concatenate([cos[mirror, :tile_width], sin[mirror, :tile_width]], axis=1)
    weight = np.full(h, 2.0)
    weight[0] = 1.0
    weight[-1] = 1.0
    final = np.concatenate(
        [cos[:tile_width, :h] * weight, -2.0 * sin[:tile_width, 1:h - 1]], axis=1
    ) / (n * n)
    as32 = lambda a: jnp.asarray(a.astype(np.float32))
    return tuple(as32(a) for a in (left, left_t, right_w, right_t, back, final))


def per_device(micrograph, templates, defocus_values, defocus_group):
    tile_rows, tile_width = micrograph.shape
    margin = TPL // 2
    n = tile_width + 2 * margin
    h = n // 2 + 1
    tile_count = lax.axis_size("tile")
    pixel_count = float(tile_rows * tile_width * tile_count)
    own_rows, tpl_width = templates.shape[1], templates.shape[2]
    halo = padded(micrograph, (("tile", 0),), margin)
    def lane_fold(columns):
        return sum(columns[i:i + tpl_width] for i in range(0, tile_width, tpl_width))[None, :]

    sum_row = lane_fold(jnp.sum(micrograph, axis=0))
    square_row = lane_fold(jnp.sum(micrograph * micrograph, axis=0))
    payload = jnp.concatenate([templates[0], sum_row, square_row], axis=0)
    everything = lax.all_gather(payload, "tile")
    defocus_values, defocus_group, everything = lax.optimization_barrier(
        (defocus_values, defocus_group, everything)
    )
    gathered = everything[:, :own_rows].reshape(tile_count * own_rows, tpl_width)
    ones = jnp.ones((tpl_width, tpl_width), jnp.float32)

    def lane_total(rows):
        return jnp.dot(
            jnp.sum(rows, axis=0, keepdims=True), ones,
            precision=lax.Precision.HIGHEST, preferred_element_type=jnp.float32,
        )

    centre = lane_total(everything[:, own_rows]) / pixel_count
    spread = jnp.sqrt(lane_total(everything[:, own_rows + 1]) / pixel_count - centre * centre + 1e-05)
    reps = tile_width // tpl_width
    centre, spread = jnp.tile(centre, (1, reps)), jnp.tile(spread, (1, reps))
    tile_index = lax.axis_index("tile")
    row_ids = lax.broadcasted_iota(jnp.int32, (n, 1), 0)
    valid = ((row_ids >= margin) | (tile_index > 0)) & (
        (row_ids < margin + tile_rows) | (tile_index < tile_count - 1)
    )
    rows_ext = jnp.where(valid, (halo - centre) / spread, 0.0)
    extent = gathered.shape[0]
    left, left_t, right_w, right_t, back, final = tables(tile_width, margin, extent)

    tpl_count = float(gathered.shape[0] * gathered.shape[1])
    centred = gathered - lane_total(gathered) / tpl_count
    root_mean = jnp.sqrt(lane_total(centred * centred) / tpl_count + 1e-06)
    normed = centred / (root_mean * TPL)

    edge_rows, edge_cols = ((1, 1), (0, 0)), ((0, 0), (1, 1))

    def halves(packed):
        return packed[:h], jnp.pad(packed[h:], edge_rows)

    def direct(ga, gb):
        ga_s, gb_s = jnp.pad(ga[:, h:], edge_cols), jnp.pad(gb[:, h:], edge_cols)
        return ga[:, :h] - gb_s, -(ga_s + gb[:, :h])

    def mirrored(ga, gb):
        return ga[:, 1:h - 1] + gb[:, h:], ga[:, h:] - gb[:, 1:h - 1]

    window_rows = product(left, rows_ext)
    window_rows, normed = lax.optimization_barrier((window_rows, normed))
    window_spec = product(window_rows, right_w)
    defocus_values, defocus_group, window_spec = lax.optimization_barrier(
        (defocus_values, defocus_group, window_spec)
    )
    window_parts = halves(window_spec)
    template_parts = halves(product(product(left_t, normed), right_t))

    positions = lax.iota(jnp.int32, n)
    signed_freq = (
        jnp.where(positions < n // 2, positions, positions - n).astype(jnp.float32) / n
    )
    packed_freq = jnp.where(positions < h, positions, positions - (h - 1)).astype(jnp.float32) / n
    groups = defocus_values.shape[0]
    group = defocus_group[0]
    pick_cols = lax.broadcasted_iota(jnp.int32, (groups, n), 0) == group
    defocus_cols = jnp.sum(jnp.where(pick_cols, defocus_values[:, None], 0.0), axis=0)[None, :]
    pick_rows = lax.broadcasted_iota(jnp.int32, (h, groups), 1) == group
    defocus_rows = jnp.sum(jnp.where(pick_rows, defocus_values[None, :], 0.0), axis=1)[:, None]
    phase_unit = math.pi * WAVELENGTH
    row_phase = phase_unit * defocus_rows * signed_freq[:h, None] ** 2
    col_phase = phase_unit * defocus_cols * packed_freq[None, :] ** 2
    sin_r, cos_r = jnp.sin(row_phase), jnp.cos(row_phase)
    sin_c, cos_c = jnp.sin(col_phase), jnp.cos(col_phase)
    weight_sin = math.sqrt(1.0 - AMPLITUDE * AMPLITUDE)
    col_u = weight_sin * cos_c - AMPLITUDE * sin_c
    col_v = weight_sin * sin_c + AMPLITUDE * cos_c
    contrast = -(sin_r * col_u + cos_r * col_v)
    def multiply(form, weight):
        spec_real, spec_imag = form(*window_parts)
        template_real, template_imag = form(*template_parts)
        return (
            (spec_real * template_real + spec_imag * template_imag) * weight,
            (spec_imag * template_real - spec_real * template_imag) * weight,
        )

    real_d, imag_d = multiply(direct, contrast[:, :h])
    real_m, imag_m = multiply(mirrored, contrast[:, h:])
    lhs = jnp.concatenate(
        [jnp.concatenate([real_d, real_m], axis=1), jnp.concatenate([imag_d, imag_m], axis=1)],
        axis=0,
    )
    inner = product(lhs, back)
    pr_c, pr_s = inner[:h, :tile_width], inner[:h, tile_width:]
    pi_c, pi_s = inner[h:, :tile_width], inner[h:, tile_width:]
    back_real = pr_c - pi_s
    back_imag = pr_s + pi_c
    scores = product(final, jnp.concatenate([back_real, back_imag[1:h - 1]], axis=0))

    orient_count = lax.axis_size("orient")
    share_rows = tile_rows // orient_count
    pieces = lax.all_to_all(scores, "orient", 0, 0, tiled=True).reshape(
        orient_count, share_rows, tile_width
    )
    def merge(former, latter):
        return (
            jnp.maximum(former[0], latter[0]),
            jnp.maximum(jnp.minimum(former[0], latter[0]), jnp.maximum(former[1], latter[1])),
            former[2] + latter[2],
            former[3] + latter[3],
        )

    lowest = jnp.float32(-jnp.inf)
    top, second, total, squares = lax.reduce(
        (pieces, jnp.full_like(pieces, lowest), pieces, pieces * pieces),
        (lowest, lowest, jnp.float32(0.0), jnp.float32(0.0)),
        merge,
        (0,),
    )
    mean_map = total / orient_count
    variance = squares / orient_count - mean_map * mean_map
    return (top, second, mean_map, variance)


def solution(mesh):
    placed = (P("tile", None), P("orient", "tile", None), P(), P("tile"))
    return jax.shard_map(
        per_device,
        mesh=mesh,
        in_specs=placed,
        out_specs=(
            P(("tile", "orient"), None),
            P(("tile", "orient"), None),
            P(("tile", "orient"), None),
            P(("tile", "orient"), None),
        ),
        check_vma=False,
    )
```

```python
import math

import numpy as np
import jax
import jax.numpy as jnp
from jax import lax
from jax.sharding import PartitionSpec as P

TPL = 256


WAVELENGTH = 0.0197
AMPLITUDE = 0.07
mode = lax.Precision.HIGH


def padded(shard, sides, width):
    for axis, dim in sides:
        size, length = (lax.axis_size(axis), shard.shape[dim])
        up = [(i, (i + 1) % size) for i in range(size - 1)]
        down = [(j, i) for i, j in up]
        last = lax.slice_in_dim(shard, length - width, length, axis=dim)
        initial = lax.slice_in_dim(shard, 0, width, axis=dim)
        before = lax.ppermute(last, axis, up)
        after = lax.ppermute(initial, axis, down)
        shard = jnp.concatenate([before, shard, after], axis=dim)
    return shard


def product(former, latter):
    return jnp.dot(former, latter, precision=mode, preferred_element_type=jnp.float32)


def tables(tile_width, margin, extent):
    n = tile_width + 2 * margin
    h = n // 2 + 1
    idx = np.arange(n)
    angles = 2.0 * np.pi * ((idx[:, None] * idx[None, :]) % n) / n
    cos, sin = np.cos(angles), np.sin(angles)
    left = np.concatenate([cos[:h], sin[1:h - 1]], axis=0)
    left_t = left[:, :extent]
    window_cols = slice(margin, margin + tile_width)
    right_w = np.concatenate([cos[window_cols, :h], sin[window_cols, 1:h - 1]], axis=1)
    right_t = np.concatenate([cos[:extent, :h], sin[:extent, 1:h - 1]], axis=1)
    mirror = np.concatenate([np.arange(h), n - np.arange(1, h - 1)])
    back = np.concatenate([cos[mirror, :tile_width], sin[mirror, :tile_width]], axis=1)
    weight = np.full(h, 2.0)
    weight[0] = 1.0
    weight[-1] = 1.0
    final = np.concatenate(
        [cos[:tile_width, :h] * weight, -2.0 * sin[:tile_width, 1:h - 1]], axis=1
    ) / (n * n)
    as32 = lambda a: jnp.asarray(a.astype(np.float32))
    return tuple(as32(a) for a in (left, left_t, right_w, right_t, back, final))


def per_device(micrograph, templates, defocus_values, defocus_group):
    tile_rows, tile_width = micrograph.shape
    margin = TPL // 2
    n = tile_width + 2 * margin
    h = n // 2 + 1
    tile_count = lax.axis_size("tile")
    pixel_count = float(tile_rows * tile_width * tile_count)
    own_rows, tpl_width = templates.shape[1], templates.shape[2]
    halo = padded(micrograph, (("tile", 0),), margin)
    def lane_fold(columns):
        return sum(columns[i:i + tpl_width] for i in range(0, tile_width, tpl_width))[None, :]

    sum_row = lane_fold(jnp.sum(micrograph, axis=0))
    square_row = lane_fold(jnp.sum(micrograph * micrograph, axis=0))
    payload = jnp.concatenate([templates[0], sum_row, square_row], axis=0)
    everything = lax.all_gather(payload, "tile")
    defocus_values, defocus_group, everything = lax.optimization_barrier(
        (defocus_values, defocus_group, everything)
    )
    gathered = everything[:, :own_rows].reshape(tile_count * own_rows, tpl_width)
    ones = jnp.ones((tpl_width, tpl_width), jnp.float32)

    def lane_total(rows):
        return jnp.dot(
            jnp.sum(rows, axis=0, keepdims=True), ones,
            precision=lax.Precision.HIGHEST, preferred_element_type=jnp.float32,
        )

    centre = lane_total(everything[:, own_rows]) / pixel_count
    spread = jnp.sqrt(lane_total(everything[:, own_rows + 1]) / pixel_count - centre * centre + 1e-05)
    reps = tile_width // tpl_width
    centre, spread = jnp.tile(centre, (1, reps)), jnp.tile(spread, (1, reps))
    tile_index = lax.axis_index("tile")
    row_ids = lax.broadcasted_iota(jnp.int32, (n, 1), 0)
    valid = ((row_ids >= margin) | (tile_index > 0)) & (
        (row_ids < margin + tile_rows) | (tile_index < tile_count - 1)
    )
    rows_ext = jnp.where(valid, (halo - centre) / spread, 0.0)
    extent = gathered.shape[0]
    left, left_t, right_w, right_t, back, final = tables(tile_width, margin, extent)

    tpl_count = float(gathered.shape[0] * gathered.shape[1])
    centred = gathered - lane_total(gathered) / tpl_count
    root_mean = jnp.sqrt(lane_total(centred * centred) / tpl_count + 1e-06)
    normed = centred / (root_mean * TPL)

    edge_rows, edge_cols = ((1, 1), (0, 0)), ((0, 0), (1, 1))

    def halves(packed):
        return packed[:h], jnp.pad(packed[h:], edge_rows)

    def direct(ga, gb):
        ga_s, gb_s = jnp.pad(ga[:, h:], edge_cols), jnp.pad(gb[:, h:], edge_cols)
        return ga[:, :h] - gb_s, -(ga_s + gb[:, :h])

    def mirrored(ga, gb):
        return ga[:, 1:h - 1] + gb[:, h:], ga[:, h:] - gb[:, 1:h - 1]

    window_rows = product(left, rows_ext)
    window_rows, normed = lax.optimization_barrier((window_rows, normed))
    window_parts = halves(product(window_rows, right_w))
    left_t = lax.dynamic_slice_in_dim(left, jnp.minimum(tile_index, 0), extent, axis=1)
    template_parts = halves(product(product(left_t, normed), right_t))

    positions = lax.iota(jnp.int32, n)
    signed_freq = (
        jnp.where(positions < n // 2, positions, positions - n).astype(jnp.float32) / n
    )
    packed_freq = jnp.where(positions < h, positions, positions - (h - 1)).astype(jnp.float32) / n
    groups = defocus_values.shape[0]
    group = defocus_group[0]
    pick_cols = lax.broadcasted_iota(jnp.int32, (groups, n), 0) == group
    defocus_cols = jnp.sum(jnp.where(pick_cols, defocus_values[:, None], 0.0), axis=0)[None, :]
    pick_rows = lax.broadcasted_iota(jnp.int32, (h, groups), 1) == group
    defocus_rows = jnp.sum(jnp.where(pick_rows, defocus_values[None, :], 0.0), axis=1)[:, None]
    phase_unit = math.pi * WAVELENGTH
    row_phase = phase_unit * defocus_rows * signed_freq[:h, None] ** 2
    col_phase = phase_unit * defocus_cols * packed_freq[None, :] ** 2
    sin_r, cos_r = jnp.sin(row_phase), jnp.cos(row_phase)
    sin_c, cos_c = jnp.sin(col_phase), jnp.cos(col_phase)
    weight_sin = math.sqrt(1.0 - AMPLITUDE * AMPLITUDE)
    col_u = weight_sin * cos_c - AMPLITUDE * sin_c
    col_v = weight_sin * sin_c + AMPLITUDE * cos_c
    contrast = -(sin_r * col_u + cos_r * col_v)
    def multiply(form, weight):
        spec_real, spec_imag = form(*window_parts)
        template_real, template_imag = form(*template_parts)
        return (
            (spec_real * template_real + spec_imag * template_imag) * weight,
            (spec_imag * template_real - spec_real * template_imag) * weight,
        )

    real_d, imag_d = multiply(direct, contrast[:, :h])
    real_m, imag_m = multiply(mirrored, contrast[:, h:])
    lhs = jnp.concatenate(
        [jnp.concatenate([real_d, real_m], axis=1), jnp.concatenate([imag_d, imag_m], axis=1)],
        axis=0,
    )
    inner = product(lhs, back)
    pr_c, pr_s = inner[:h, :tile_width], inner[:h, tile_width:]
    pi_c, pi_s = inner[h:, :tile_width], inner[h:, tile_width:]
    back_real = pr_c - pi_s
    back_imag = pr_s + pi_c
    scores = product(final, jnp.concatenate([back_real, back_imag[1:h - 1]], axis=0))

    orient_count = lax.axis_size("orient")
    share_rows = tile_rows // orient_count
    pieces = lax.all_to_all(scores, "orient", 0, 0, tiled=True).reshape(
        orient_count, share_rows, tile_width
    )
    def merge(former, latter):
        return (
            jnp.maximum(former[0], latter[0]),
            jnp.maximum(jnp.minimum(former[0], latter[0]), jnp.maximum(former[1], latter[1])),
            former[2] + latter[2],
            former[3] + latter[3],
        )

    lowest = jnp.float32(-jnp.inf)
    top, second, total, squares = lax.reduce(
        (pieces, jnp.full_like(pieces, lowest), pieces, pieces * pieces),
        (lowest, lowest, jnp.float32(0.0), jnp.float32(0.0)),
        merge,
        (0,),
    )
    mean_map = total / orient_count
    variance = squares / orient_count - mean_map * mean_map
    return (top, second, mean_map, variance)


def solution(mesh):
    placed = (P("tile", None), P("orient", "tile", None), P(), P("tile"))
    return jax.shard_map(
        per_device,
        mesh=mesh,
        in_specs=placed,
        out_specs=(
            P(("tile", "orient"), None),
            P(("tile", "orient"), None),
            P(("tile", "orient"), None),
            P(("tile", "orient"), None),
        ),
        check_vma=False,
    )
```

```python
import math

import numpy as np
import jax
import jax.numpy as jnp
from jax import lax
from jax.sharding import PartitionSpec as P

TPL = 256


WAVELENGTH = 0.0197
AMPLITUDE = 0.07
mode = lax.Precision.HIGH


def padded(shard, sides, width):
    for axis, dim in sides:
        size, length = (lax.axis_size(axis), shard.shape[dim])
        up = [(i, (i + 1) % size) for i in range(size - 1)]
        down = [(j, i) for i, j in up]
        last = lax.slice_in_dim(shard, length - width, length, axis=dim)
        initial = lax.slice_in_dim(shard, 0, width, axis=dim)
        before = lax.ppermute(last, axis, up)
        after = lax.ppermute(initial, axis, down)
        shard = jnp.concatenate([before, shard, after], axis=dim)
    return shard


def product(former, latter):
    return jnp.dot(former, latter, precision=mode, preferred_element_type=jnp.float32)


def tables(tile_width, margin, extent):
    n = tile_width + 2 * margin
    h = n // 2 + 1
    idx = np.arange(n)
    angles = 2.0 * np.pi * ((idx[:, None] * idx[None, :]) % n) / n
    cos, sin = np.cos(angles), np.sin(angles)
    left = np.concatenate([cos[:h], sin[1:h - 1]], axis=0)
    left_t = left[:, :extent]
    window_cols = slice(margin, margin + tile_width)
    right_w = np.concatenate([cos[window_cols, :h], sin[window_cols, 1:h - 1]], axis=1)
    right_t = np.concatenate([cos[:extent, :h], sin[:extent, 1:h - 1]], axis=1)
    mirror = np.concatenate([np.arange(h), n - np.arange(1, h - 1)])
    back = np.concatenate([cos[mirror, :tile_width], sin[mirror, :tile_width]], axis=1)
    weight = np.full(h, 2.0)
    weight[0] = 1.0
    weight[-1] = 1.0
    final = np.concatenate(
        [cos[:tile_width, :h] * weight, -2.0 * sin[:tile_width, 1:h - 1]], axis=1
    ) / (n * n)
    as32 = lambda a: jnp.asarray(a.astype(np.float32))
    return tuple(as32(a) for a in (left, left_t, right_w, right_t, back, final))


def per_device(micrograph, templates, defocus_values, defocus_group):
    tile_rows, tile_width = micrograph.shape
    margin = TPL // 2
    n = tile_width + 2 * margin
    h = n // 2 + 1
    tile_count = lax.axis_size("tile")
    pixel_count = float(tile_rows * tile_width * tile_count)
    own_rows, tpl_width = templates.shape[1], templates.shape[2]
    halo = padded(micrograph, (("tile", 0),), margin)
    def lane_fold(columns):
        return sum(columns[i:i + tpl_width] for i in range(0, tile_width, tpl_width))[None, :]

    sum_row = lane_fold(jnp.sum(micrograph, axis=0))
    square_row = lane_fold(jnp.sum(micrograph * micrograph, axis=0))
    payload = jnp.concatenate([templates[0], sum_row, square_row], axis=0)
    everything = lax.all_gather(payload, "tile")
    defocus_values, defocus_group, everything = lax.optimization_barrier(
        (defocus_values, defocus_group, everything)
    )
    gathered = everything[:, :own_rows].reshape(tile_count * own_rows, tpl_width)
    ones = jnp.ones((tpl_width, tpl_width), jnp.float32)

    def lane_total(rows):
        return jnp.dot(
            jnp.sum(rows, axis=0, keepdims=True), ones,
            precision=lax.Precision.HIGHEST, preferred_element_type=jnp.float32,
        )

    centre = lane_total(everything[:, own_rows]) / pixel_count
    spread = jnp.sqrt(lane_total(everything[:, own_rows + 1]) / pixel_count - centre * centre + 1e-05)
    reps = tile_width // tpl_width
    centre, spread = jnp.tile(centre, (1, reps)), jnp.tile(spread, (1, reps))
    tile_index = lax.axis_index("tile")
    row_ids = lax.broadcasted_iota(jnp.int32, (n, 1), 0)
    valid = ((row_ids >= margin) | (tile_index > 0)) & (
        (row_ids < margin + tile_rows) | (tile_index < tile_count - 1)
    )
    rows_ext = jnp.where(valid, (halo - centre) / spread, 0.0)
    extent = gathered.shape[0]
    left, left_t, right_w, right_t, back, final = tables(tile_width, margin, extent)

    tpl_count = float(gathered.shape[0] * gathered.shape[1])
    centred = gathered - lane_total(gathered) / tpl_count
    root_mean = jnp.sqrt(lane_total(centred * centred) / tpl_count + 1e-06)
    normed = centred / (root_mean * TPL)

    edge_rows, edge_cols = ((1, 1), (0, 0)), ((0, 0), (1, 1))

    def halves(packed):
        return packed[:h], jnp.pad(packed[h:], edge_rows)

    def direct(ga, gb):
        ga_s, gb_s = jnp.pad(ga[:, h:], edge_cols), jnp.pad(gb[:, h:], edge_cols)
        return ga[:, :h] - gb_s, -(ga_s + gb[:, :h])

    def mirrored(ga, gb):
        return ga[:, 1:h - 1] + gb[:, h:], ga[:, h:] - gb[:, 1:h - 1]

    window_rows = product(left, rows_ext)
    window_rows, normed = lax.optimization_barrier((window_rows, normed))
    window_parts = halves(product(window_rows, right_w))
    normed_rows = jnp.pad(normed, ((0, n - extent), (0, 0)))
    template_parts = halves(product(product(left, normed_rows), right_t))

    positions = lax.iota(jnp.int32, n)
    signed_freq = (
        jnp.where(positions < n // 2, positions, positions - n).astype(jnp.float32) / n
    )
    packed_freq = jnp.where(positions < h, positions, positions - (h - 1)).astype(jnp.float32) / n
    groups = defocus_values.shape[0]
    group = defocus_group[0]
    pick_cols = lax.broadcasted_iota(jnp.int32, (groups, n), 0) == group
    defocus_cols = jnp.sum(jnp.where(pick_cols, defocus_values[:, None], 0.0), axis=0)[None, :]
    pick_rows = lax.broadcasted_iota(jnp.int32, (h, groups), 1) == group
    defocus_rows = jnp.sum(jnp.where(pick_rows, defocus_values[None, :], 0.0), axis=1)[:, None]
    phase_unit = math.pi * WAVELENGTH
    row_phase = phase_unit * defocus_rows * signed_freq[:h, None] ** 2
    col_phase = phase_unit * defocus_cols * packed_freq[None, :] ** 2
    sin_r, cos_r = jnp.sin(row_phase), jnp.cos(row_phase)
    sin_c, cos_c = jnp.sin(col_phase), jnp.cos(col_phase)
    weight_sin = math.sqrt(1.0 - AMPLITUDE * AMPLITUDE)
    col_u = weight_sin * cos_c - AMPLITUDE * sin_c
    col_v = weight_sin * sin_c + AMPLITUDE * cos_c
    contrast = -(sin_r * col_u + cos_r * col_v)
    def multiply(form, weight):
        spec_real, spec_imag = form(*window_parts)
        template_real, template_imag = form(*template_parts)
        return (
            (spec_real * template_real + spec_imag * template_imag) * weight,
            (spec_imag * template_real - spec_real * template_imag) * weight,
        )

    real_d, imag_d = multiply(direct, contrast[:, :h])
    real_m, imag_m = multiply(mirrored, contrast[:, h:])
    lhs = jnp.concatenate(
        [jnp.concatenate([real_d, real_m], axis=1), jnp.concatenate([imag_d, imag_m], axis=1)],
        axis=0,
    )
    inner = product(lhs, back)
    pr_c, pr_s = inner[:h, :tile_width], inner[:h, tile_width:]
    pi_c, pi_s = inner[h:, :tile_width], inner[h:, tile_width:]
    back_real = pr_c - pi_s
    back_imag = pr_s + pi_c
    scores = product(final, jnp.concatenate([back_real, back_imag[1:h - 1]], axis=0))

    orient_count = lax.axis_size("orient")
    share_rows = tile_rows // orient_count
    pieces = lax.all_to_all(scores, "orient", 0, 0, tiled=True).reshape(
        orient_count, share_rows, tile_width
    )
    def merge(former, latter):
        return (
            jnp.maximum(former[0], latter[0]),
            jnp.maximum(jnp.minimum(former[0], latter[0]), jnp.maximum(former[1], latter[1])),
            former[2] + latter[2],
            former[3] + latter[3],
        )

    lowest = jnp.float32(-jnp.inf)
    top, second, total, squares = lax.reduce(
        (pieces, jnp.full_like(pieces, lowest), pieces, pieces * pieces),
        (lowest, lowest, jnp.float32(0.0), jnp.float32(0.0)),
        merge,
        (0,),
    )
    mean_map = total / orient_count
    variance = squares / orient_count - mean_map * mean_map
    return (top, second, mean_map, variance)


def solution(mesh):
    placed = (P("tile", None), P("orient", "tile", None), P(), P("tile"))
    return jax.shard_map(
        per_device,
        mesh=mesh,
        in_specs=placed,
        out_specs=(
            P(("tile", "orient"), None),
            P(("tile", "orient"), None),
            P(("tile", "orient"), None),
            P(("tile", "orient"), None),
        ),
        check_vma=False,
    )
```
